32 devices in a mesh: fsdp: 16 (over z, x, core), tp: 2 (over y).
Axes of the slice: x: 2, y: 2, z: 4, core: 2. Of those that a mesh axis runs over, the one named last changes fastest.
Arguments:
- xbc: bfloat16 [4096, 8, 2304], P('fsdp', 'tp'), may hold values from -6 to 6
- dt_raw: bfloat16 [256, 4096], P('tp', 'fsdp'), may hold values from -3 to 3
- conv_weight: bfloat16 [4, 8, 2304], P(None, 'tp'), may hold values from -3 to 3
- conv_bias: bfloat16 [8, 2304], P('tp'), may hold values from -3 to 3
- dt_bias: float32 [256], P('tp'), may hold values from -13 to 0
- a_log: float32 [256], P('tp'), may hold values from -1.5 to -0.1
- d_skip: float32 [256], P('tp'), may hold values from 0.5 to 1.5
Outputs:
- mixed: float32 [4096, 16384], P(('fsdp', 'tp'))
The draws below stay inside these ranges and needn't reach their ends.
All inputs are finite; a program needn't handle non-finite values.
Results may differ from the reference program's by a relative error of at most 0.0016.
Values may be sent and summed in bfloat16 or wider, within the bound.
No kernel may reach another device: no remote copies, remote signals or barrier semaphores. Data moves between devices by JAX's collectives and lax.ppermute only.
A program may use at most 256 MiB of HBM per device.

```python
import math
import jax
import jax.numpy as jnp
from jax import lax

GROUPS = 8
HEAD_DIM = 64
STATE = 128
CONV = 4
ROWS_DEV = 256
HEADS = 256
GROUP_CH = 2304
L = 4096


def head_kinds(key):
    base = jax.random.fold_in(key, 71)
    pick_key, rate_key, reach_key = jax.random.split(base, 3)
    slow_share = 0.5
    middle_share = 0.4
    picked = jax.random.uniform(pick_key, (HEADS,))
    spread = jax.random.uniform(rate_key, (HEADS,), minval=-1.0, maxval=1.0)
    a_values = -0.8 + 0.7 * spread
    reach = jax.random.uniform(reach_key, (HEADS,))
    slow_target = math.log(0.1) + reach * math.log(8.0) - math.log(L)
    middle_target = math.log(0.1) + reach * math.log(40.0) - math.log(ROWS_DEV)
    fast_target = math.log(0.02) + reach * math.log(2.0)
    target = jnp.where(picked < slow_share, slow_target, jnp.where(picked < slow_share + middle_share, middle_target, fast_target))
    bias_values = jnp.clip(target - a_values - math.log(1.22), -13.0, 0.0)
    return (a_values.astype(jnp.float32), bias_values.astype(jnp.float32))


def draw_a_log(key, part):
    return head_kinds(key)[0]


def draw_dt_bias(key, part):
    return head_kinds(key)[1]


def draw_dt_raw(key, part):
    noise_key, offset_key = jax.random.split(jax.random.fold_in(key, 11))
    block_count = L // ROWS_DEV
    noise = 0.5 * jax.random.normal(noise_key, (HEADS, L))
    offsets = jax.random.uniform(offset_key, (HEADS, block_count), minval=-0.7, maxval=0.7)
    summed = noise + jnp.repeat(offsets, ROWS_DEV, axis=1)
    return jnp.clip(summed, -3.0, 3.0).astype(jnp.bfloat16)


def levels(stream_key, dims, cuts, low, largest):
    def one(position, parts):
        draws = jax.random.uniform(jax.random.fold_in(jax.random.fold_in(stream_key, 6), position), (parts,), jnp.float32, low / len(cuts), largest / len(cuts))
        return jnp.repeat(jnp.exp(draws), dims[position] // parts).reshape((-1,) + (1,) * (len(dims) - position - 1))

    factor_of = one(*cuts[0])
    for cut in cuts[1:]:
        factor_of = factor_of * one(*cut)
    return factor_of


def normal_values(stream_key, shape, scale, most, shards=(), kind=jnp.bfloat16):
    drawn = jax.random.normal(stream_key, shape, jnp.float32) * scale
    if len(shards) > 0:
        drawn = levels(stream_key, shape, shards, -0.22, 0.18) * drawn
    return jnp.clip(drawn, min=-most, max=most).astype(kind)


def setup_inputs(seed: int = 0) -> dict:
    streams_of = jax.random.split(jax.random.key(seed), 8)
    xbc = normal_values(streams_of[0], (L, GROUPS, GROUP_CH), 1.0, 6.0, ((0, 16), (1, 2)))
    dt_raw = draw_dt_raw(jax.random.fold_in(streams_of[7], 71), 0)
    conv_weight = normal_values(streams_of[2], (CONV, GROUPS, GROUP_CH), CONV ** -0.5, 3.0, ((1, 2),))
    conv_bias = normal_values(streams_of[3], (GROUPS, GROUP_CH), 0.5, 3.0, ((0, 2),))
    dt_bias = draw_dt_bias(jax.random.fold_in(streams_of[7], 71), 0)
    a_log = draw_a_log(jax.random.fold_in(streams_of[7], 71), 0)
    d_skip = jnp.clip(0.5 + 1.0 * jax.random.uniform(streams_of[6], (HEADS,), jnp.float32) ** levels(streams_of[6], (HEADS,), ((0, 2),), -0.2, 0.2), 0.5, 1.5)
    return dict(xbc=xbc, dt_raw=dt_raw, conv_weight=conv_weight, conv_bias=conv_bias, dt_bias=dt_bias, a_log=a_log, d_skip=d_skip)


def reference(xbc, dt_raw, conv_weight, conv_bias, dt_bias, a_log, d_skip):
    seq_len, group_count, channel_count = xbc.shape
    head_count = dt_raw.shape[0]
    per_group = head_count // group_count
    inner_width = per_group * HEAD_DIM
    block_rows = math.gcd(seq_len, 128)
    block_count = seq_len // block_rows
    step_sizes = jax.nn.softplus(dt_raw.astype(jnp.float32) + dt_bias[:, None])
    log_rates = -jnp.exp(a_log)[:, None] * step_sizes

    def blocks_of(arr):
        return jnp.moveaxis(arr.reshape(group_count, per_group, block_count, block_rows), 2, 0)

    raw_blocks = xbc.reshape(block_count, block_rows, group_count, channel_count)
    skip_grouped = d_skip.reshape(group_count, per_group)
    causal = lax.broadcasted_iota(jnp.int32, (block_rows, block_rows), 0) >= lax.broadcasted_iota(jnp.int32, (block_rows, block_rows), 1)
    exact = lax.Precision.HIGHEST

    def advance(carry, pieces):
        states, tail = carry
        raw, step_blk, rate_blk = pieces
        padded = jnp.concatenate([tail, raw], axis=0)
        summed = conv_bias.astype(jnp.float32)[None]
        for k in range(CONV):
            summed = summed + conv_weight[k].astype(jnp.float32)[None] * padded[k:k + block_rows].astype(jnp.float32)
        activated = jax.nn.silu(summed).astype(jnp.bfloat16)
        values = activated[:, :, :inner_width].astype(jnp.float32).reshape(block_rows, group_count, per_group, HEAD_DIM)
        b_part = activated[:, :, inner_width:inner_width + STATE].astype(jnp.float32)
        c_part = activated[:, :, inner_width + STATE:].astype(jnp.float32)
        scores = jnp.einsum("tgn,sgn->gts", c_part, b_part, precision=exact)
        cum_log = jnp.cumsum(rate_blk, axis=2)
        gaps = cum_log[:, :, :, None] - cum_log[:, :, None, :]
        decays = jnp.exp(jnp.where(causal, gaps, -jnp.inf))
        mixing = decays * scores[:, None] * step_blk[:, :, None, :]
        output = jnp.einsum("gjts,sgjp->tgjp", mixing, values, precision=exact)
        carried = jnp.einsum("tgn,gjnp->tgjp", c_part, states, precision=exact)
        output = output + jnp.transpose(jnp.exp(cum_log), (2, 0, 1))[..., None] * carried
        output = output + skip_grouped[None, :, :, None] * values
        ending = cum_log[:, :, -1:]
        weights = jnp.exp(ending - cum_log) * step_blk
        weighted = values * jnp.transpose(weights, (2, 0, 1))[..., None]
        added = jnp.einsum("sgn,sgjp->gjnp", b_part, weighted, precision=exact)
        states = jnp.exp(ending)[..., None] * states + added
        new_tail = raw[block_rows - (CONV - 1):]
        return (states, new_tail), output.reshape(block_rows, head_count * HEAD_DIM)

    initial = (jnp.zeros((group_count, per_group, STATE, HEAD_DIM), jnp.float32),
               jnp.zeros((CONV - 1, group_count, channel_count), xbc.dtype))
    final_carry, outputs = lax.scan(advance, initial, (raw_blocks, blocks_of(step_sizes), blocks_of(log_rates)))
    return outputs.reshape(seq_len, head_count * HEAD_DIM)
```

```python
import jax
import jax.numpy as jnp
from jax import lax
from jax.sharding import Mesh, PartitionSpec as P

HEAD_DIM = 64
STATE = 128
SEQ = ("fh", "fl")


def convolve(xbc, conv_weight, conv_bias, seq_count):
    row_count = xbc.shape[0]
    tap_count = conv_weight.shape[0]
    rim = xbc[row_count - (tap_count - 1) :]
    rim_rows = lax.ppermute(rim, SEQ, [(d, d + 1) for d in range(seq_count - 1)])
    padded = jnp.concatenate([rim_rows, xbc], axis=0)
    summed = conv_bias.astype(jnp.float32)[None]
    for k in range(tap_count):
        summed = summed + conv_weight[k].astype(jnp.float32)[None] * padded[
            k : k + row_count
        ].astype(jnp.float32)
    return jax.nn.silu(summed).astype(jnp.bfloat16)


def shards(xbc, dt_raw, conv_weight, conv_bias, dt_bias, a_log, d_skip, seq_count):
    row_count, group_count, _ = xbc.shape
    head_count = dt_raw.shape[0]
    per_group = head_count // group_count
    inner_width = per_group * HEAD_DIM
    exact = lax.Precision.HIGHEST
    f32 = jnp.float32

    activated = convolve(xbc, conv_weight, conv_bias, seq_count)
    chunk = min(128, row_count)
    nck = row_count // chunk
    values = activated[:, :, :inner_width].reshape(nck, chunk, group_count, per_group, HEAD_DIM)
    b_part = activated[:, :, inner_width : inner_width + STATE].reshape(nck, chunk, group_count, STATE)
    c_part = activated[:, :, inner_width + STATE :].reshape(nck, chunk, group_count, STATE)

    step_sizes = jax.nn.softplus(dt_raw.astype(f32) + dt_bias[:, None])
    log_rates = -jnp.exp(a_log)[:, None] * step_sizes
    steps = step_sizes.reshape(group_count, per_group, nck, chunk)
    rates = log_rates.reshape(group_count, per_group, nck, chunk)
    cum = jnp.cumsum(rates, axis=3)
    chunk_log = cum[..., -1]

    causal = lax.broadcasted_iota(jnp.int32, (chunk, chunk), 0) >= lax.broadcasted_iota(
        jnp.int32, (chunk, chunk), 1
    )
    scores = jnp.einsum("ktgn,ksgn->kgts", c_part, b_part, preferred_element_type=f32)
    gaps = cum[..., :, None] - cum[..., None, :]
    decays = jnp.exp(jnp.where(causal, gaps, -jnp.inf))
    mixing = decays * jnp.transpose(scores, (1, 0, 2, 3))[:, None] * steps[..., None, :]
    values32 = values.astype(f32)
    output = jnp.einsum("gjkts,ksgjp->ktgjp", mixing, values32, precision=exact)
    output = output + d_skip.reshape(group_count, per_group)[None, None, :, :, None] * values32

    weights = jnp.exp(chunk_log[..., None] - cum) * steps
    weighted = values32 * jnp.transpose(weights, (2, 3, 0, 1))[..., None]
    chunk_states = jnp.einsum("ksgn,ksgjp->kgjnp", b_part.astype(f32), weighted, precision=exact)

    kk = jnp.arange(nck)
    between = (kk[None, :, None] < kk[None, None, :]) & (kk[None, None, :] < kk[:, None, None])
    gap_log = jnp.einsum("kam,gjm->gjka", between.astype(f32), chunk_log)
    pre_w = jnp.where((kk[None, :] < kk[:, None])[None, None], jnp.exp(gap_log), 0.0)
    local_in = jnp.einsum("gjka,agjnp->kgjnp", pre_w, chunk_states, precision=exact)
    cum_dev = cum + jnp.concatenate(
        [jnp.zeros_like(chunk_log[..., :1]), jnp.cumsum(chunk_log, axis=2)[..., :-1]], axis=2
    )[..., None]
    dev_log = jnp.sum(chunk_log, axis=2)
    later = (kk[:, None] < kk[None, :]).astype(f32)
    after_w = jnp.exp(jnp.einsum("km,gjm->gjk", later, chunk_log))
    dev_state = jnp.einsum("gjk,kgjnp->gjnp", after_w, chunk_states, precision=exact)

    carried_local = jnp.einsum("ktgn,kgjnp->ktgjp", c_part.astype(f32), local_in, precision=exact)
    output = output + jnp.transpose(jnp.exp(cum), (2, 3, 0, 1))[..., None] * carried_local

    lo = lax.axis_index("fl")
    hi = lax.axis_index("fh")
    pair_count = seq_count // 2
    half = per_group // 2
    all_log = lax.all_gather(dev_log, SEQ)
    first_log = all_log[2 * hi]
    second_log = all_log[2 * hi + 1]
    own_half = lax.dynamic_slice_in_dim(dev_state, lo * half, half, axis=1)
    other_half = lax.dynamic_slice_in_dim(dev_state, (1 - lo) * half, half, axis=1)
    swap = [(0, 1), (1, 0)]
    recv_a = lax.ppermute(other_half, "fl", swap)
    first_state = jnp.where(lo == 0, own_half, recv_a)
    second_state = jnp.where(lo == 0, recv_a, own_half)
    second_log_half = lax.dynamic_slice_in_dim(second_log, lo * half, half, axis=1)
    first_log_half = lax.dynamic_slice_in_dim(first_log, lo * half, half, axis=1)
    pair_state = jnp.exp(second_log_half)[..., None, None] * first_state + second_state
    gathered = lax.all_gather(pair_state, "fh")

    pair_log = all_log.reshape(pair_count, 2, group_count, per_group).sum(axis=1)
    pair_log_half = lax.dynamic_slice_in_dim(pair_log, lo * half, half, axis=2)
    pp = jnp.arange(pair_count)
    strictly = (pp[:, None] < pp[None, :]) & (pp[None, :] < hi)
    gap = jnp.einsum("am,mgj->agj", strictly.astype(f32), pair_log_half)
    pair_w = jnp.where((pp < hi)[:, None, None], jnp.exp(gap), 0.0)
    pair_in = jnp.einsum("agj,agjnp->gjnp", pair_w, gathered, precision=exact)

    first_decay = jnp.exp(first_log_half)[..., None, None]
    own_in = jnp.where(lo == 0, pair_in, first_decay * pair_in + recv_a)
    sent = jnp.where(lo == 0, first_decay * pair_in + own_half, pair_in)
    recv_c = lax.ppermute(sent, "fl", swap)
    incoming = jnp.where(
        lo == 0,
        jnp.concatenate([own_in, recv_c], axis=1),
        jnp.concatenate([recv_c, own_in], axis=1),
    )

    carried = jnp.einsum("ktgn,gjnp->ktgjp", c_part.astype(f32), incoming, precision=exact)
    output = output + jnp.transpose(jnp.exp(cum_dev), (2, 3, 0, 1))[..., None] * carried
    merged = output.reshape(row_count, head_count * HEAD_DIM)
    return lax.all_to_all(merged, "tp", split_axis=0, concat_axis=1, tiled=True)


def solution(mesh):
    seq_count = mesh.shape["fsdp"]
    tp_count = mesh.shape["tp"]
    grid = Mesh(mesh.devices.reshape(seq_count // 2, 2, tp_count), ("fh", "fl", "tp"))
    in_specs = (
        P(SEQ, "tp", None),
        P("tp", SEQ),
        P(None, "tp", None),
        P("tp", None),
        P("tp"),
        P("tp"),
        P("tp"),
    )
    out_specs = P(SEQ + ("tp",), None)

    def body(*args):
        return shards(*args, seq_count=seq_count)

    return jax.shard_map(body, mesh=grid, in_specs=in_specs, out_specs=out_specs, check_vma=False)
```

```python
import jax
import jax.numpy as jnp
from jax import lax
from jax.sharding import Mesh, PartitionSpec as P

HEAD_DIM = 64
STATE = 128
SEQ = ("fh", "fl")


def convolve(xbc, conv_weight, conv_bias, seq_count):
    row_count = xbc.shape[0]
    tap_count = conv_weight.shape[0]
    rim = xbc[row_count - (tap_count - 1) :]
    rim_rows = lax.ppermute(rim, SEQ, [(d, d + 1) for d in range(seq_count - 1)])
    padded = jnp.concatenate([rim_rows, xbc], axis=0)
    summed = conv_bias.astype(jnp.float32)[None]
    for k in range(tap_count):
        summed = summed + conv_weight[k].astype(jnp.float32)[None] * padded[
            k : k + row_count
        ].astype(jnp.float32)
    return jax.nn.silu(summed).astype(jnp.bfloat16)


def shards(xbc, dt_raw, conv_weight, conv_bias, dt_bias, a_log, d_skip, seq_count, tp_count):
    row_count, group_count, _ = xbc.shape
    head_count = dt_raw.shape[0]
    per_group = head_count // group_count
    inner_width = per_group * HEAD_DIM
    exact = lax.Precision.HIGHEST
    f32 = jnp.float32

    activated = convolve(xbc, conv_weight, conv_bias, seq_count)
    chunk = min(128, row_count)
    nck = row_count // chunk
    values = activated[:, :, :inner_width].reshape(nck, chunk, group_count, per_group, HEAD_DIM)
    b_part = activated[:, :, inner_width : inner_width + STATE].reshape(nck, chunk, group_count, STATE)
    c_part = activated[:, :, inner_width + STATE :].reshape(nck, chunk, group_count, STATE)

    step_sizes = jax.nn.softplus(dt_raw.astype(f32) + dt_bias[:, None])
    log_rates = -jnp.exp(a_log)[:, None] * step_sizes
    steps = step_sizes.reshape(group_count, per_group, nck, chunk)
    rates = log_rates.reshape(group_count, per_group, nck, chunk)
    cum = jnp.cumsum(rates, axis=3)
    chunk_log = cum[..., -1]

    causal = lax.broadcasted_iota(jnp.int32, (chunk, chunk), 0) >= lax.broadcasted_iota(
        jnp.int32, (chunk, chunk), 1
    )
    scores = jnp.einsum("ktgn,ksgn->kgts", c_part, b_part, preferred_element_type=f32)
    gaps = cum[..., :, None] - cum[..., None, :]
    decays = jnp.exp(jnp.where(causal, gaps, -jnp.inf))
    mixing = decays * jnp.transpose(scores, (1, 0, 2, 3))[:, None] * steps[..., None, :]
    values32 = values.astype(f32)
    output = jnp.einsum("gjkts,ksgjp->ktgjp", mixing, values32, precision=exact)
    output = output + d_skip.reshape(group_count, per_group)[None, None, :, :, None] * values32

    weights = jnp.exp(chunk_log[..., None] - cum) * steps
    weighted = values32 * jnp.transpose(weights, (2, 3, 0, 1))[..., None]
    chunk_states = jnp.einsum("ksgn,ksgjp->kgjnp", b_part.astype(f32), weighted, precision=exact)

    kk = jnp.arange(nck)
    between = (kk[None, :, None] < kk[None, None, :]) & (kk[None, None, :] < kk[:, None, None])
    gap_log = jnp.einsum("kam,gjm->gjka", between.astype(f32), chunk_log, precision=exact)
    pre_w = jnp.where((kk[None, :] < kk[:, None])[None, None], jnp.exp(gap_log), 0.0)
    local_in = jnp.einsum("gjka,agjnp->kgjnp", pre_w, chunk_states, precision=exact)
    cum_dev = cum + jnp.concatenate(
        [jnp.zeros_like(chunk_log[..., :1]), jnp.cumsum(chunk_log, axis=2)[..., :-1]], axis=2
    )[..., None]
    dev_log = jnp.sum(chunk_log, axis=2)
    later = (kk[:, None] < kk[None, :]).astype(f32)
    after_w = jnp.exp(jnp.einsum("km,gjm->gjk", later, chunk_log, precision=exact))
    dev_state = jnp.einsum("gjk,kgjnp->gjnp", after_w, chunk_states, precision=exact)

    carried_local = jnp.einsum("ktgn,kgjnp->ktgjp", c_part.astype(f32), local_in, precision=exact)
    output = output + jnp.transpose(jnp.exp(cum), (2, 3, 0, 1))[..., None] * carried_local

    lo = lax.axis_index("fl")
    hi = lax.axis_index("fh")
    pair_count = seq_count // 2
    half = per_group // 2
    swap = [(0, 1), (1, 0)]
    partner_log = lax.ppermute(dev_log, "fl", swap)
    first_log = jnp.where(lo == 0, dev_log, partner_log)
    second_log = jnp.where(lo == 0, partner_log, dev_log)
    own_half = lax.dynamic_slice_in_dim(dev_state, lo * half, half, axis=1)
    other_half = lax.dynamic_slice_in_dim(dev_state, (1 - lo) * half, half, axis=1)
    recv_a = lax.ppermute(other_half, "fl", swap)
    first_state = jnp.where(lo == 0, own_half, recv_a)
    second_state = jnp.where(lo == 0, recv_a, own_half)
    second_log_half = lax.dynamic_slice_in_dim(second_log, lo * half, half, axis=1)
    first_log_half = lax.dynamic_slice_in_dim(first_log, lo * half, half, axis=1)
    pair_state = jnp.exp(second_log_half)[..., None, None] * first_state + second_state
    pair_log_half = first_log_half + second_log_half
    pair_in = exclusive_scan(pair_state, pair_log_half, hi, pair_count)

    first_decay = jnp.exp(first_log_half)[..., None, None]
    own_in = jnp.where(lo == 0, pair_in, first_decay * pair_in + recv_a)
    sent = jnp.where(lo == 0, first_decay * pair_in + own_half, pair_in)
    recv_c = lax.ppermute(sent, "fl", swap)
    incoming = jnp.where(
        lo == 0,
        jnp.concatenate([own_in, recv_c], axis=1),
        jnp.concatenate([recv_c, own_in], axis=1),
    )

    carried = jnp.einsum("ktgn,gjnp->ktgjp", c_part.astype(f32), incoming, precision=exact)
    output = output + jnp.transpose(jnp.exp(cum_dev), (2, 3, 0, 1))[..., None] * carried
    return exchange_rows(output.reshape(row_count, head_count * HEAD_DIM), tp_count)


def exclusive_scan(state, log_decay, mine, count):
    def shifted(value, step):
        return lax.ppermute(value, "fh", [(d, d + step) for d in range(count - step)])

    def pack(st, lg):
        return jnp.concatenate([st, jnp.broadcast_to(lg[..., None, None], st.shape[:2] + (1, st.shape[3]))], axis=2)

    packed = shifted(pack(state, log_decay), 1)
    cur_s, cur_a = packed[:, :, :STATE], packed[:, :, STATE, 0]
    step = 1
    while step < count:
        got = shifted(pack(cur_s, cur_a), step)
        take = mine >= step
        new_s = jnp.exp(cur_a)[..., None, None] * got[:, :, :STATE] + cur_s
        new_a = got[:, :, STATE, 0] + cur_a
        cur_s = jnp.where(take, new_s, cur_s)
        cur_a = jnp.where(take, new_a, cur_a)
        step *= 2
    return cur_s


def exchange_rows(merged, tp_count):
    mine = lax.axis_index("tp")
    rows = merged.shape[0] // tp_count
    blocks = merged.reshape(tp_count, rows, merged.shape[1])
    pieces = [None] * tp_count
    for shift in range(tp_count):
        sent = lax.dynamic_index_in_dim(blocks, (mine + shift) % tp_count, 0, keepdims=False)
        if shift == 0:
            got = sent
        else:
            got = lax.ppermute(sent, "tp", [(d, (d + shift) % tp_count) for d in range(tp_count)])
        pieces[shift] = got
    placed = []
    for column in range(tp_count):
        value = pieces[0]
        for shift in range(1, tp_count):
            value = jnp.where((mine - shift) % tp_count == column, pieces[shift], value)
        placed.append(value)
    return jnp.concatenate(placed, axis=1)


def solution(mesh):
    seq_count = mesh.shape["fsdp"]
    tp_count = mesh.shape["tp"]
    grid = Mesh(mesh.devices.reshape(seq_count // 2, 2, tp_count), ("fh", "fl", "tp"))
    in_specs = (
        P(SEQ, "tp", None),
        P("tp", SEQ),
        P(None, "tp", None),
        P("tp", None),
        P("tp"),
        P("tp"),
        P("tp"),
    )
    out_specs = P(SEQ + ("tp",), None)

    def body(*args):
        return shards(*args, seq_count=seq_count, tp_count=tp_count)

    return jax.shard_map(body, mesh=grid, in_specs=in_specs, out_specs=out_specs, check_vma=False)
```

```python
import jax
import jax.numpy as jnp
from jax import lax
from jax.sharding import Mesh, PartitionSpec as P

HEAD_DIM = 64
STATE = 128
SEQ = ("fh", "fl")


def convolve(xbc, conv_weight, conv_bias, seq_count):
    row_count = xbc.shape[0]
    tap_count = conv_weight.shape[0]
    rim = xbc[row_count - (tap_count - 1) :]
    rim_rows = lax.ppermute(rim, SEQ, [(d, d + 1) for d in range(seq_count - 1)])
    padded = jnp.concatenate([rim_rows, xbc], axis=0)
    summed = conv_bias.astype(jnp.float32)[None]
    for k in range(tap_count):
        summed = summed + conv_weight[k].astype(jnp.float32)[None] * padded[
            k : k + row_count
        ].astype(jnp.float32)
    return jax.nn.silu(summed).astype(jnp.bfloat16)


def shards(xbc, dt_raw, conv_weight, conv_bias, dt_bias, a_log, d_skip, seq_count, tp_count):
    row_count, group_count, _ = xbc.shape
    head_count = dt_raw.shape[0]
    per_group = head_count // group_count
    inner_width = per_group * HEAD_DIM
    exact = lax.Precision.HIGHEST
    f32 = jnp.float32

    activated = convolve(xbc, conv_weight, conv_bias, seq_count)
    chunk = min(128, row_count)
    nck = row_count // chunk
    values = activated[:, :, :inner_width].reshape(nck, chunk, group_count, per_group, HEAD_DIM)
    b_part = activated[:, :, inner_width : inner_width + STATE].reshape(nck, chunk, group_count, STATE)
    c_part = activated[:, :, inner_width + STATE :].reshape(nck, chunk, group_count, STATE)

    step_sizes = jax.nn.softplus(dt_raw.astype(f32) + dt_bias[:, None])
    log_rates = -jnp.exp(a_log)[:, None] * step_sizes
    steps = step_sizes.reshape(group_count, per_group, nck, chunk)
    rates = log_rates.reshape(group_count, per_group, nck, chunk)
    cum = jnp.cumsum(rates, axis=3)
    chunk_log = cum[..., -1]

    values32 = values.astype(f32)
    weights = jnp.exp(chunk_log[..., None] - cum) * steps
    weighted = values32 * jnp.transpose(weights, (2, 3, 0, 1))[..., None]
    chunk_states = jnp.einsum("ksgn,ksgjp->kgjnp", b_part.astype(f32), weighted, precision=exact)

    running = jnp.zeros_like(chunk_states[0])
    local_list = []
    for k in range(nck):
        local_list.append(running)
        running = jnp.exp(chunk_log[:, :, k])[..., None, None] * running + chunk_states[k]
    local_in = jnp.stack(local_list, axis=0)
    dev_state = running
    cum_dev = cum + jnp.concatenate(
        [jnp.zeros_like(chunk_log[..., :1]), jnp.cumsum(chunk_log, axis=2)[..., :-1]], axis=2
    )[..., None]
    dev_log = jnp.sum(chunk_log, axis=2)

    def intra(side):
        values32, b_part, c_part, local_in = side
        causal = lax.broadcasted_iota(jnp.int32, (chunk, chunk), 0) >= lax.broadcasted_iota(
            jnp.int32, (chunk, chunk), 1
        )
        scores = jnp.einsum("ktgn,ksgn->kgts", c_part, b_part, preferred_element_type=f32)
        gaps = cum[..., :, None] - cum[..., None, :]
        decays = jnp.exp(jnp.where(causal, gaps, -jnp.inf))
        mixing = decays * jnp.transpose(scores, (1, 0, 2, 3))[:, None] * steps[..., None, :]
        output = jnp.einsum("gjkts,ksgjp->ktgjp", mixing, values32, precision=exact)
        output = output + d_skip.reshape(group_count, per_group)[None, None, :, :, None] * values32

        carried_local = jnp.einsum("ktgn,kgjnp->ktgjp", c_part.astype(f32), local_in, precision=exact)
        return output + jnp.transpose(jnp.exp(cum), (2, 3, 0, 1))[..., None] * carried_local

    lo = lax.axis_index("fl")
    hi = lax.axis_index("fh")
    pair_count = seq_count // 2
    half = per_group // 2
    swap = [(0, 1), (1, 0)]
    partner_log = lax.ppermute(dev_log, "fl", swap)
    first_log = jnp.where(lo == 0, dev_log, partner_log)
    second_log = jnp.where(lo == 0, partner_log, dev_log)
    own_half = lax.dynamic_slice_in_dim(dev_state, lo * half, half, axis=1)
    other_half = lax.dynamic_slice_in_dim(dev_state, (1 - lo) * half, half, axis=1)
    recv_a = lax.ppermute(other_half, "fl", swap)
    first_state = jnp.where(lo == 0, own_half, recv_a)
    second_state = jnp.where(lo == 0, recv_a, own_half)
    second_log_half = lax.dynamic_slice_in_dim(second_log, lo * half, half, axis=1)
    first_log_half = lax.dynamic_slice_in_dim(first_log, lo * half, half, axis=1)
    pair_state = jnp.exp(second_log_half)[..., None, None] * first_state + second_state
    pair_log_half = first_log_half + second_log_half
    pair_in, output = exclusive_scan(
        pair_state, pair_log_half, hi, pair_count, (values32, b_part, c_part, local_in), intra
    )

    first_decay = jnp.exp(first_log_half)[..., None, None]
    own_in = jnp.where(lo == 0, pair_in, first_decay * pair_in + recv_a)
    sent = jnp.where(lo == 0, first_decay * pair_in + own_half, pair_in)
    recv_c = lax.ppermute(sent, "fl", swap)
    incoming = jnp.where(
        lo == 0,
        jnp.concatenate([own_in, recv_c], axis=1),
        jnp.concatenate([recv_c, own_in], axis=1),
    )

    carried = jnp.einsum("ktgn,gjnp->ktgjp", c_part.astype(f32), incoming, precision=exact)
    output = output + jnp.transpose(jnp.exp(cum_dev), (2, 3, 0, 1))[..., None] * carried
    return exchange_rows(output.reshape(row_count, head_count * HEAD_DIM), tp_count)


def exclusive_scan(state, log_decay, mine, count, side, work):
    shape = state.shape
    width = 1024

    def shifted(value, step):
        return lax.ppermute(value, "fh", [(d, d + step) for d in range(count - step)])

    def pack(st, lg):
        flat_log = jnp.pad(lg.reshape(1, -1), ((0, 0), (0, width - lg.size)))
        return jnp.concatenate([st.reshape(-1, width), flat_log], axis=0)

    def unpack(packed):
        return packed[:-1].reshape(shape), packed[-1, : log_decay.size].reshape(log_decay.shape)

    first, side = lax.optimization_barrier((pack(state, log_decay), side))
    got = shifted(first, 1)
    done = work(side)
    got, done = lax.optimization_barrier((got, done))
    cur_s, cur_a = unpack(got)
    step = 1
    while step < count:
        got_s, got_a = unpack(shifted(pack(cur_s, cur_a), step))
        take = mine >= step
        new_s = jnp.exp(cur_a)[..., None, None] * got_s + cur_s
        new_a = got_a + cur_a
        cur_s = jnp.where(take, new_s, cur_s)
        cur_a = jnp.where(take, new_a, cur_a)
        step *= 2
    return cur_s, done


def exchange_rows(merged, tp_count):
    mine = lax.axis_index("tp")
    rows = merged.shape[0] // tp_count
    blocks = merged.reshape(tp_count, rows, merged.shape[1])
    pieces = [None] * tp_count
    for shift in range(tp_count):
        sent = lax.dynamic_index_in_dim(blocks, (mine + shift) % tp_count, 0, keepdims=False)
        if shift == 0:
            got = sent
        else:
            got = lax.ppermute(sent, "tp", [(d, (d + shift) % tp_count) for d in range(tp_count)])
        pieces[shift] = got
    placed = []
    for column in range(tp_count):
        value = pieces[0]
        for shift in range(1, tp_count):
            value = jnp.where((mine - shift) % tp_count == column, pieces[shift], value)
        placed.append(value)
    return jnp.concatenate(placed, axis=1)


def solution(mesh):
    seq_count = mesh.shape["fsdp"]
    tp_count = mesh.shape["tp"]
    grid = Mesh(mesh.devices.reshape(seq_count // 2, 2, tp_count), ("fh", "fl", "tp"))
    in_specs = (
        P(SEQ, "tp", None),
        P("tp", SEQ),
        P(None, "tp", None),
        P("tp", None),
        P("tp"),
        P("tp"),
        P("tp"),
    )
    out_specs = P(SEQ + ("tp",), None)

    def body(*args):
        return shards(*args, seq_count=seq_count, tp_count=tp_count)

    return jax.shard_map(body, mesh=grid, in_specs=in_specs, out_specs=out_specs, check_vma=False)
```

```python
import jax
import jax.numpy as jnp
from jax import lax
from jax.sharding import Mesh, PartitionSpec as P

HEAD_DIM = 64
STATE = 128
SEQ = ("fh", "fl")


def convolve(xbc, conv_weight, conv_bias, seq_count):
    row_count = xbc.shape[0]
    tap_count = conv_weight.shape[0]
    rim = xbc[row_count - (tap_count - 1) :]
    rim_rows = lax.ppermute(rim, SEQ, [(d, d + 1) for d in range(seq_count - 1)])
    padded = jnp.concatenate([rim_rows, xbc], axis=0)
    summed = conv_bias.astype(jnp.float32)[None]
    for k in range(tap_count):
        summed = summed + conv_weight[k].astype(jnp.float32)[None] * padded[
            k : k + row_count
        ].astype(jnp.float32)
    return jax.nn.silu(summed).astype(jnp.bfloat16)


def shards(xbc, dt_raw, conv_weight, conv_bias, dt_bias, a_log, d_skip, seq_count, tp_count):
    row_count, group_count, _ = xbc.shape
    head_count = dt_raw.shape[0]
    per_group = head_count // group_count
    inner_width = per_group * HEAD_DIM
    exact = lax.Precision.HIGHEST
    f32 = jnp.float32

    activated = convolve(xbc, conv_weight, conv_bias, seq_count)
    chunk = min(128, row_count)
    nck = row_count // chunk
    values = activated[:, :, :inner_width].reshape(nck, chunk, group_count, per_group, HEAD_DIM)
    b_part = activated[:, :, inner_width : inner_width + STATE].reshape(nck, chunk, group_count, STATE)
    c_part = activated[:, :, inner_width + STATE :].reshape(nck, chunk, group_count, STATE)

    step_sizes = jax.nn.softplus(dt_raw.astype(f32) + dt_bias[:, None])
    log_rates = -jnp.exp(a_log)[:, None] * step_sizes
    steps = step_sizes.reshape(group_count, per_group, nck, chunk)
    rates = log_rates.reshape(group_count, per_group, nck, chunk)
    cum = jnp.cumsum(rates, axis=3)
    chunk_log = cum[..., -1]

    values32 = values.astype(f32)
    weights = jnp.exp(chunk_log[..., None] - cum) * steps
    weighted = values32 * jnp.transpose(weights, (2, 3, 0, 1))[..., None]
    chunk_states = jnp.einsum("ksgn,ksgjp->kgjnp", b_part.astype(f32), weighted, precision=exact)

    running = jnp.zeros_like(chunk_states[0])
    local_list = []
    for k in range(nck):
        local_list.append(running)
        running = jnp.exp(chunk_log[:, :, k])[..., None, None] * running + chunk_states[k]
    local_in = jnp.stack(local_list, axis=0)
    dev_state = running
    cum_dev = cum + jnp.concatenate(
        [jnp.zeros_like(chunk_log[..., :1]), jnp.cumsum(chunk_log, axis=2)[..., :-1]], axis=2
    )[..., None]
    dev_log = jnp.sum(chunk_log, axis=2)

    def intra(side):
        values32, b_part, c_part, local_in = side
        causal = lax.broadcasted_iota(jnp.int32, (chunk, chunk), 0) >= lax.broadcasted_iota(
            jnp.int32, (chunk, chunk), 1
        )
        scores = jnp.einsum("ktgn,ksgn->kgts", c_part, b_part, preferred_element_type=f32)
        gaps = cum[..., :, None] - cum[..., None, :]
        decays = jnp.exp(jnp.where(causal, gaps, -jnp.inf))
        mixing = decays * jnp.transpose(scores, (1, 0, 2, 3))[:, None] * steps[..., None, :]
        output = jnp.einsum("gjkts,ksgjp->ktgjp", mixing, values32, precision=exact)
        output = output + d_skip.reshape(group_count, per_group)[None, None, :, :, None] * values32

        carried_local = jnp.einsum("ktgn,kgjnp->ktgjp", c_part.astype(f32), local_in, precision=exact)
        return output + jnp.transpose(jnp.exp(cum), (2, 3, 0, 1))[..., None] * carried_local

    lo = lax.axis_index("fl")
    hi = lax.axis_index("fh")
    pair_count = seq_count // 2
    half = per_group // 2
    swap = [(0, 1), (1, 0)]
    partner_log = lax.ppermute(dev_log, "fl", swap)
    first_log = jnp.where(lo == 0, dev_log, partner_log)
    second_log = jnp.where(lo == 0, partner_log, dev_log)
    own_half = lax.dynamic_slice_in_dim(dev_state, lo * half, half, axis=1)
    other_half = lax.dynamic_slice_in_dim(dev_state, (1 - lo) * half, half, axis=1)
    recv_a = lax.ppermute(other_half, "fl", swap)
    first_state = jnp.where(lo == 0, own_half, recv_a)
    second_state = jnp.where(lo == 0, recv_a, own_half)
    second_log_half = lax.dynamic_slice_in_dim(second_log, lo * half, half, axis=1)
    first_log_half = lax.dynamic_slice_in_dim(first_log, lo * half, half, axis=1)
    pair_state = jnp.exp(second_log_half)[..., None, None] * first_state + second_state
    pair_log_half = first_log_half + second_log_half
    pair_in, output = exclusive_scan(
        pair_state, pair_log_half, hi, pair_count, (values32, b_part, c_part, local_in), intra
    )

    first_decay = jnp.exp(first_log_half)[..., None, None]
    own_in = jnp.where(lo == 0, pair_in, first_decay * pair_in + recv_a)
    sent = jnp.where(lo == 0, first_decay * pair_in + own_half, pair_in)
    recv_c = lax.ppermute(sent, "fl", swap)
    incoming = jnp.where(
        lo == 0,
        jnp.concatenate([own_in, recv_c], axis=1),
        jnp.concatenate([recv_c, own_in], axis=1),
    )

    carried = jnp.einsum("ktgn,gjnp->ktgjp", c_part.astype(f32), incoming, precision=exact)
    output = output + jnp.transpose(jnp.exp(cum_dev), (2, 3, 0, 1))[..., None] * carried
    return exchange_rows(output.reshape(row_count, head_count * HEAD_DIM), tp_count)


def exclusive_scan(state, log_decay, mine, count, side, work):
    shape = state.shape
    width = 1024
    heads = log_decay.size
    per_head = state.size // heads // width

    def shifted(value, step):
        return lax.ppermute(value, "fh", [(d, d + step) for d in range(count - step)])

    def combine(got, cur):
        scale = jnp.repeat(jnp.exp(cur[-1, :heads]), per_head)[:, None]
        body = scale * got[:-1] + cur[:-1]
        logs = got[-1:] + cur[-1:]
        return jnp.concatenate([body, logs], axis=0)

    flat_log = jnp.pad(log_decay.reshape(1, -1), ((0, 0), (0, width - heads)))
    first = jnp.concatenate([state.reshape(-1, width), flat_log], axis=0)
    first, side = lax.optimization_barrier((first, side))
    cur = shifted(first, 1)
    done = work(side)
    cur, done = lax.optimization_barrier((cur, done))
    step = 1
    while step < count:
        cur = jnp.where(mine >= step, combine(shifted(cur, step), cur), cur)
        step *= 2
    return cur[:-1].reshape(shape), done


def exchange_rows(merged, tp_count):
    mine = lax.axis_index("tp")
    rows = merged.shape[0] // tp_count
    blocks = merged.reshape(tp_count, rows, merged.shape[1])
    pieces = [None] * tp_count
    for shift in range(tp_count):
        sent = lax.dynamic_index_in_dim(blocks, (mine + shift) % tp_count, 0, keepdims=False)
        if shift == 0:
            got = sent
        else:
            got = lax.ppermute(sent, "tp", [(d, (d + shift) % tp_count) for d in range(tp_count)])
        pieces[shift] = got
    placed = []
    for column in range(tp_count):
        value = pieces[0]
        for shift in range(1, tp_count):
            value = jnp.where((mine - shift) % tp_count == column, pieces[shift], value)
        placed.append(value)
    return jnp.concatenate(placed, axis=1)


def solution(mesh):
    seq_count = mesh.shape["fsdp"]
    tp_count = mesh.shape["tp"]
    grid = Mesh(mesh.devices.reshape(seq_count // 2, 2, tp_count), ("fh", "fl", "tp"))
    in_specs = (
        P(SEQ, "tp", None),
        P("tp", SEQ),
        P(None, "tp", None),
        P("tp", None),
        P("tp"),
        P("tp"),
        P("tp"),
    )
    out_specs = P(SEQ + ("tp",), None)

    def body(*args):
        return shards(*args, seq_count=seq_count, tp_count=tp_count)

    return jax.shard_map(body, mesh=grid, in_specs=in_specs, out_specs=out_specs, check_vma=False)
```

```python
import jax
import jax.numpy as jnp
from jax import lax
from jax.sharding import Mesh, PartitionSpec as P

HEAD_DIM = 64
STATE = 128
SEQ = ("fh", "fl")


def convolve(xbc, conv_weight, conv_bias, seq_count):
    row_count = xbc.shape[0]
    tap_count = conv_weight.shape[0]
    rim = xbc[row_count - (tap_count - 1) :]
    rim_rows = lax.ppermute(rim, SEQ, [(d, d + 1) for d in range(seq_count - 1)])
    padded = jnp.concatenate([rim_rows, xbc], axis=0)
    summed = conv_bias.astype(jnp.float32)[None]
    for k in range(tap_count):
        summed = summed + conv_weight[k].astype(jnp.float32)[None] * padded[
            k : k + row_count
        ].astype(jnp.float32)
    return jax.nn.silu(summed).astype(jnp.bfloat16)


def shards(xbc, dt_raw, conv_weight, conv_bias, dt_bias, a_log, d_skip, seq_count, tp_count):
    row_count, group_count, _ = xbc.shape
    head_count = dt_raw.shape[0]
    per_group = head_count // group_count
    inner_width = per_group * HEAD_DIM
    exact = lax.Precision.HIGHEST
    f32 = jnp.float32

    activated = convolve(xbc, conv_weight, conv_bias, seq_count)
    chunk = min(128, row_count)
    nck = row_count // chunk
    values = activated[:, :, :inner_width].reshape(nck, chunk, group_count, per_group, HEAD_DIM)
    b_part = activated[:, :, inner_width : inner_width + STATE].reshape(nck, chunk, group_count, STATE)
    c_part = activated[:, :, inner_width + STATE :].reshape(nck, chunk, group_count, STATE)

    step_sizes = jax.nn.softplus(dt_raw.astype(f32) + dt_bias[:, None])
    log_rates = -jnp.exp(a_log)[:, None] * step_sizes
    steps = step_sizes.reshape(group_count, per_group, nck, chunk)
    rates = log_rates.reshape(group_count, per_group, nck, chunk)
    cum = jnp.cumsum(rates, axis=3)
    chunk_log = cum[..., -1]

    values32 = values.astype(f32)
    weights = jnp.exp(chunk_log[..., None] - cum) * steps
    weighted = values32 * jnp.transpose(weights, (2, 3, 0, 1))[..., None]
    chunk_states = jnp.einsum("ksgn,ksgjp->kgjpn", b_part.astype(f32), weighted, precision=exact)

    running = jnp.zeros_like(chunk_states[0])
    local_list = []
    for k in range(nck):
        local_list.append(running)
        running = jnp.exp(chunk_log[:, :, k])[..., None, None] * running + chunk_states[k]
    dev_state = running
    cum_dev = cum + jnp.concatenate(
        [jnp.zeros_like(chunk_log[..., :1]), jnp.cumsum(chunk_log, axis=2)[..., :-1]], axis=2
    )[..., None]
    dev_log = jnp.sum(chunk_log, axis=2)

    def intra(side):
        values32, b_part, c_part, local_list = side
        causal = lax.broadcasted_iota(jnp.int32, (chunk, chunk), 0) >= lax.broadcasted_iota(
            jnp.int32, (chunk, chunk), 1
        )
        scores = jnp.einsum("ktgn,ksgn->kgts", c_part, b_part, preferred_element_type=f32)
        gaps = cum[..., :, None] - cum[..., None, :]
        decays = jnp.exp(jnp.where(causal, gaps, -jnp.inf))
        mixing = decays * jnp.transpose(scores, (1, 0, 2, 3))[:, None] * steps[..., None, :]
        output = jnp.einsum("gjkts,ksgjp->ktgjp", mixing, values32, precision=exact)
        output = output + d_skip.reshape(group_count, per_group)[None, None, :, :, None] * values32

        if nck == 1:
            return output
        later = jnp.stack(local_list[1:], axis=0)
        carried_local = jnp.einsum("ktgn,kgjpn->ktgjp", c_part[1:].astype(f32), later, precision=exact)
        scale = jnp.transpose(jnp.exp(cum[:, :, 1:]), (2, 3, 0, 1))[..., None]
        return jnp.concatenate([output[:1], output[1:] + scale * carried_local], axis=0)

    lo = lax.axis_index("fl")
    hi = lax.axis_index("fh")
    pair_count = seq_count // 2
    half = per_group // 2
    swap = [(0, 1), (1, 0)]
    partner_log = lax.ppermute(dev_log, "fl", swap)
    first_log = jnp.where(lo == 0, dev_log, partner_log)
    second_log = jnp.where(lo == 0, partner_log, dev_log)
    own_half = lax.dynamic_slice_in_dim(dev_state, lo * half, half, axis=1)
    other_half = lax.dynamic_slice_in_dim(dev_state, (1 - lo) * half, half, axis=1)
    recv_a = lax.ppermute(other_half, "fl", swap)
    first_state = jnp.where(lo == 0, own_half, recv_a)
    second_state = jnp.where(lo == 0, recv_a, own_half)
    second_log_half = lax.dynamic_slice_in_dim(second_log, lo * half, half, axis=1)
    first_log_half = lax.dynamic_slice_in_dim(first_log, lo * half, half, axis=1)
    pair_state = jnp.exp(second_log_half)[..., None, None] * first_state + second_state
    pair_log_half = first_log_half + second_log_half
    pair_in, output = exclusive_scan(
        pair_state, pair_log_half, hi, pair_count, (values32, b_part, c_part, local_list), intra
    )

    first_decay = jnp.exp(first_log_half)[..., None, None]
    own_in = jnp.where(lo == 0, pair_in, first_decay * pair_in + recv_a)
    sent = jnp.where(lo == 0, first_decay * pair_in + own_half, pair_in)
    recv_c = lax.ppermute(sent, "fl", swap)
    incoming = jnp.where(
        lo == 0,
        jnp.concatenate([own_in, recv_c], axis=1),
        jnp.concatenate([recv_c, own_in], axis=1),
    )

    carried = jnp.einsum("ktgn,gjpn->ktgjp", c_part.astype(f32), incoming, precision=exact)
    output = output + jnp.transpose(jnp.exp(cum_dev), (2, 3, 0, 1))[..., None] * carried
    return exchange_rows(output.reshape(row_count, head_count * HEAD_DIM), tp_count)


def exclusive_scan(state, log_decay, mine, count, side, work):
    shape = state.shape
    width = state.shape[-1]
    heads = log_decay.size
    per_head = state.size // heads // width
    log_rows = -(-heads // width)

    def shifted(value, step):
        return lax.ppermute(value, "fh", [(d, d + step) for d in range(count - step)])

    def combine(got, cur):
        scale = jnp.repeat(jnp.exp(cur[-log_rows:].reshape(-1)[:heads]), per_head)[:, None]
        body = scale * got[:-log_rows] + cur[:-log_rows]
        logs = got[-log_rows:] + cur[-log_rows:]
        return jnp.concatenate([body, logs], axis=0)

    flat_log = jnp.pad(log_decay.reshape(-1), (0, log_rows * width - heads)).reshape(log_rows, width)
    first = jnp.concatenate([state.reshape(-1, width), flat_log], axis=0)
    first, side = lax.optimization_barrier((first, side))
    cur = shifted(first, 1)
    done = work(side)
    cur, done = lax.optimization_barrier((cur, done))
    step = 1
    while step < count:
        cur = jnp.where(mine >= step, combine(shifted(cur, step), cur), cur)
        step *= 2
    return cur[:-log_rows].reshape(shape), done


def exchange_rows(merged, tp_count):
    mine = lax.axis_index("tp")
    rows = merged.shape[0] // tp_count
    blocks = merged.reshape(tp_count, rows, merged.shape[1])
    pieces = [None] * tp_count
    for shift in range(tp_count):
        sent = lax.dynamic_index_in_dim(blocks, (mine + shift) % tp_count, 0, keepdims=False)
        if shift == 0:
            got = sent
        else:
            got = lax.ppermute(sent, "tp", [(d, (d + shift) % tp_count) for d in range(tp_count)])
        pieces[shift] = got
    placed = []
    for column in range(tp_count):
        value = pieces[0]
        for shift in range(1, tp_count):
            value = jnp.where((mine - shift) % tp_count == column, pieces[shift], value)
        placed.append(value)
    return jnp.concatenate(placed, axis=1)


def solution(mesh):
    seq_count = mesh.shape["fsdp"]
    tp_count = mesh.shape["tp"]
    grid = Mesh(mesh.devices.reshape(seq_count // 2, 2, tp_count), ("fh", "fl", "tp"))
    in_specs = (
        P(SEQ, "tp", None),
        P("tp", SEQ),
        P(None, "tp", None),
        P("tp", None),
        P("tp"),
        P("tp"),
        P("tp"),
    )
    out_specs = P(SEQ + ("tp",), None)

    def body(*args):
        return shards(*args, seq_count=seq_count, tp_count=tp_count)

    return jax.shard_map(body, mesh=grid, in_specs=in_specs, out_specs=out_specs, check_vma=False)
```

```python
import jax
import jax.numpy as jnp
from jax import lax
from jax.sharding import Mesh, PartitionSpec as P

HEAD_DIM = 64
STATE = 128
SEQ = ("fh", "fl")


def convolve(xbc, conv_weight, conv_bias, seq_count):
    row_count = xbc.shape[0]
    tap_count = conv_weight.shape[0]
    rim = xbc[row_count - (tap_count - 1) :]
    rim_rows = lax.ppermute(rim, SEQ, [(d, d + 1) for d in range(seq_count - 1)])
    padded = jnp.concatenate([rim_rows, xbc], axis=0)
    summed = conv_bias.astype(jnp.float32)[None]
    for k in range(tap_count):
        summed = summed + conv_weight[k].astype(jnp.float32)[None] * padded[
            k : k + row_count
        ].astype(jnp.float32)
    return jax.nn.silu(summed).astype(jnp.bfloat16)


def shards(xbc, dt_raw, conv_weight, conv_bias, dt_bias, a_log, d_skip, seq_count, tp_count):
    row_count, group_count, _ = xbc.shape
    head_count = dt_raw.shape[0]
    per_group = head_count // group_count
    inner_width = per_group * HEAD_DIM
    exact = lax.Precision.HIGHEST
    f32 = jnp.float32

    activated = convolve(xbc, conv_weight, conv_bias, seq_count)
    chunk = min(128, row_count)
    nck = row_count // chunk
    values = activated[:, :, :inner_width].reshape(nck, chunk, group_count, per_group, HEAD_DIM)
    b_part = activated[:, :, inner_width : inner_width + STATE].reshape(nck, chunk, group_count, STATE)
    c_part = activated[:, :, inner_width + STATE :].reshape(nck, chunk, group_count, STATE)

    step_sizes = jax.nn.softplus(dt_raw.astype(f32) + dt_bias[:, None])
    log_rates = -jnp.exp(a_log)[:, None] * step_sizes
    steps = step_sizes.reshape(group_count, per_group, nck, chunk)
    rates = log_rates.reshape(group_count, per_group, nck, chunk)
    cum = jnp.cumsum(rates, axis=3)
    chunk_log = cum[..., -1]

    values32 = values.astype(f32)
    weights = jnp.exp(chunk_log[..., None] - cum) * steps
    weighted = values32 * jnp.transpose(weights, (2, 3, 0, 1))[..., None]
    chunk_states = jnp.einsum("ksgn,ksgjp->kgjpn", b_part.astype(f32), weighted, precision=exact)

    running = jnp.zeros_like(chunk_states[0])
    local_list = []
    for k in range(nck):
        local_list.append(running)
        running = jnp.exp(chunk_log[:, :, k])[..., None, None] * running + chunk_states[k]
    dev_state = running
    cum_dev = cum + jnp.concatenate(
        [jnp.zeros_like(chunk_log[..., :1]), jnp.cumsum(chunk_log, axis=2)[..., :-1]], axis=2
    )[..., None]
    dev_log = jnp.sum(chunk_log, axis=2)

    def intra(side):
        values32, b_part, c_part, local_list = side
        causal = lax.broadcasted_iota(jnp.int32, (chunk, chunk), 0) >= lax.broadcasted_iota(
            jnp.int32, (chunk, chunk), 1
        )
        scores = jnp.einsum("ktgn,ksgn->kgts", c_part, b_part, preferred_element_type=f32)
        gaps = cum[..., :, None] - cum[..., None, :]
        decays = jnp.exp(jnp.where(causal, gaps, -jnp.inf))
        mixing = decays * jnp.transpose(scores, (1, 0, 2, 3))[:, None] * steps[..., None, :]
        output = jnp.einsum("gjkts,ksgjp->ktgjp", mixing, values32, precision=exact)
        output = output + d_skip.reshape(group_count, per_group)[None, None, :, :, None] * values32

        if nck == 1:
            return output
        later = jnp.stack(local_list[1:], axis=0)
        carried_local = jnp.einsum("ktgn,kgjpn->ktgjp", c_part[1:].astype(f32), later, precision=exact)
        scale = jnp.transpose(jnp.exp(cum[:, :, 1:]), (2, 3, 0, 1))[..., None]
        return jnp.concatenate([output[:1], output[1:] + scale * carried_local], axis=0)

    lo = lax.axis_index("fl")
    hi = lax.axis_index("fh")
    pair_count = seq_count // 2
    half = per_group // 2
    swap = [(0, 1), (1, 0)]
    partner_log = lax.ppermute(dev_log, "fl", swap)
    first_log = jnp.where(lo == 0, dev_log, partner_log)
    second_log = jnp.where(lo == 0, partner_log, dev_log)
    own_half = lax.dynamic_slice_in_dim(dev_state, lo * half, half, axis=1)
    other_half = lax.dynamic_slice_in_dim(dev_state, (1 - lo) * half, half, axis=1)
    recv_a = lax.ppermute(other_half, "fl", swap)
    first_state = jnp.where(lo == 0, own_half, recv_a)
    second_state = jnp.where(lo == 0, recv_a, own_half)
    second_log_half = lax.dynamic_slice_in_dim(second_log, lo * half, half, axis=1)
    first_log_half = lax.dynamic_slice_in_dim(first_log, lo * half, half, axis=1)
    pair_state = jnp.exp(second_log_half)[..., None, None] * first_state + second_state
    pair_log_half = first_log_half + second_log_half
    quarter = half // 2
    c32 = c_part.astype(f32)
    first_decay = jnp.exp(first_log_half)[..., None, None]
    grow = jnp.exp(cum_dev).reshape(group_count, 2, 2, quarter, nck, chunk)

    def finish(pair_in, q, intra_out):
        part = slice(q * quarter, (q + 1) * quarter)
        own_in = jnp.where(lo == 0, pair_in, first_decay[:, part] * pair_in + recv_a[:, part])
        sent = jnp.where(lo == 0, first_decay[:, part] * pair_in + own_half[:, part], pair_in)
        recv_c = lax.ppermute(sent, "fl", swap)
        incoming = jnp.where(
            lo == 0, jnp.stack([own_in, recv_c], axis=1), jnp.stack([recv_c, own_in], axis=1)
        )
        carried = jnp.einsum("ktgn,ghrpn->ktghrp", c32, incoming, precision=exact)
        scale = jnp.transpose(grow[:, :, q], (3, 4, 0, 1, 2))[..., None]
        base = intra_out.reshape(nck, chunk, group_count, 2, 2, quarter, HEAD_DIM)[:, :, :, :, q]
        return (base + scale * carried).reshape(row_count, -1)

    first_in, output = exclusive_scan(
        pair_state[:, :quarter], pair_log_half[:, :quarter], hi, pair_count,
        (values32, b_part, c_part, local_list), intra,
    )

    def first_rows(side):
        first_in, output = side
        return finish(first_in, 0, output)

    second_in, first_piece = exclusive_scan(
        pair_state[:, quarter:], pair_log_half[:, quarter:], hi, pair_count,
        (first_in, output), first_rows,
    )
    sent_first = exchange_rows(first_piece, tp_count)
    sent_second = exchange_rows(finish(second_in, 1, output), tp_count)
    rows = row_count // tp_count
    both = [
        piece.reshape(rows, tp_count, group_count, 2, quarter, HEAD_DIM)
        for piece in (sent_first, sent_second)
    ]
    return jnp.stack(both, axis=4).reshape(rows, tp_count * head_count * HEAD_DIM)


def exclusive_scan(state, log_decay, mine, count, side, work):
    shape = state.shape
    width = state.shape[-1]
    heads = log_decay.size
    per_head = state.size // heads // width
    log_rows = -(-heads // width)

    def shifted(value, step):
        return lax.ppermute(value, "fh", [(d, d + step) for d in range(count - step)])

    def combine(got, cur):
        scale = jnp.repeat(jnp.exp(cur[-log_rows:].reshape(-1)[:heads]), per_head)[:, None]
        body = scale * got[:-log_rows] + cur[:-log_rows]
        logs = got[-log_rows:] + cur[-log_rows:]
        return jnp.concatenate([body, logs], axis=0)

    flat_log = jnp.pad(log_decay.reshape(-1), (0, log_rows * width - heads)).reshape(log_rows, width)
    first = jnp.concatenate([state.reshape(-1, width), flat_log], axis=0)
    first, side = lax.optimization_barrier((first, side))
    cur = shifted(first, 1)
    done = work(side)
    cur, done = lax.optimization_barrier((cur, done))
    step = 1
    while step < count:
        got = shifted(cur, step)
        cur = jnp.where(mine >= step, combine(got, cur), cur)
        step *= 2
    return cur[:-log_rows].reshape(shape), done


def exchange_rows(merged, tp_count):
    mine = lax.axis_index("tp")
    rows = merged.shape[0] // tp_count
    blocks = merged.reshape(tp_count, rows, merged.shape[1])
    pieces = [None] * tp_count
    for shift in range(tp_count):
        sent = lax.dynamic_index_in_dim(blocks, (mine + shift) % tp_count, 0, keepdims=False)
        if shift == 0:
            got = sent
        else:
            got = lax.ppermute(sent, "tp", [(d, (d + shift) % tp_count) for d in range(tp_count)])
        pieces[shift] = got
    placed = []
    for column in range(tp_count):
        value = pieces[0]
        for shift in range(1, tp_count):
            value = jnp.where((mine - shift) % tp_count == column, pieces[shift], value)
        placed.append(value)
    return jnp.concatenate(placed, axis=1)


def solution(mesh):
    seq_count = mesh.shape["fsdp"]
    tp_count = mesh.shape["tp"]
    grid = Mesh(mesh.devices.reshape(seq_count // 2, 2, tp_count), ("fh", "fl", "tp"))
    in_specs = (
        P(SEQ, "tp", None),
        P("tp", SEQ),
        P(None, "tp", None),
        P("tp", None),
        P("tp"),
        P("tp"),
        P("tp"),
    )
    out_specs = P(SEQ + ("tp",), None)

    def body(*args):
        return shards(*args, seq_count=seq_count, tp_count=tp_count)

    return jax.shard_map(body, mesh=grid, in_specs=in_specs, out_specs=out_specs, check_vma=False)
```

```python
import jax
import jax.numpy as jnp
from jax import lax
from jax.sharding import Mesh, PartitionSpec as P

HEAD_DIM = 64
STATE = 128
SEQ = ("fh", "fl")


def convolve(xbc, conv_weight, conv_bias, seq_count):
    row_count = xbc.shape[0]
    tap_count = conv_weight.shape[0]
    rim = xbc[row_count - (tap_count - 1) :]
    rim_rows = lax.ppermute(rim, SEQ, [(d, d + 1) for d in range(seq_count - 1)])
    padded = jnp.concatenate([rim_rows, xbc], axis=0)
    summed = conv_bias.astype(jnp.float32)[None]
    for k in range(tap_count):
        summed = summed + conv_weight[k].astype(jnp.float32)[None] * padded[
            k : k + row_count
        ].astype(jnp.float32)
    return jax.nn.silu(summed).astype(jnp.bfloat16)


def shards(xbc, dt_raw, conv_weight, conv_bias, dt_bias, a_log, d_skip, seq_count, tp_count):
    row_count, group_count, _ = xbc.shape
    head_count = dt_raw.shape[0]
    per_group = head_count // group_count
    inner_width = per_group * HEAD_DIM
    exact = lax.Precision.HIGHEST
    f32 = jnp.float32

    activated = convolve(xbc, conv_weight, conv_bias, seq_count)
    chunk = min(128, row_count)
    nck = row_count // chunk
    values = activated[:, :, :inner_width].reshape(nck, chunk, group_count, per_group, HEAD_DIM)
    b_part = activated[:, :, inner_width : inner_width + STATE].reshape(nck, chunk, group_count, STATE)
    c_part = activated[:, :, inner_width + STATE :].reshape(nck, chunk, group_count, STATE)

    step_sizes = jax.nn.softplus(dt_raw.astype(f32) + dt_bias[:, None])
    log_rates = -jnp.exp(a_log)[:, None] * step_sizes
    steps = step_sizes.reshape(group_count, per_group, nck, chunk)
    rates = log_rates.reshape(group_count, per_group, nck, chunk)
    cum = jnp.cumsum(rates, axis=3)
    chunk_log = cum[..., -1]

    values32 = values.astype(f32)
    weights = jnp.exp(chunk_log[..., None] - cum) * steps
    weighted = values32 * jnp.transpose(weights, (2, 3, 0, 1))[..., None]
    chunk_states = jnp.einsum("ksgn,ksgjp->kgjpn", b_part.astype(f32), weighted, precision=exact)

    running = jnp.zeros_like(chunk_states[0])
    local_list = []
    for k in range(nck):
        local_list.append(running)
        running = jnp.exp(chunk_log[:, :, k])[..., None, None] * running + chunk_states[k]
    dev_state = running
    cum_dev = cum + jnp.concatenate(
        [jnp.zeros_like(chunk_log[..., :1]), jnp.cumsum(chunk_log, axis=2)[..., :-1]], axis=2
    )[..., None]
    dev_log = jnp.sum(chunk_log, axis=2)

    def intra(side):
        values32, b_part, c_part, local_list = side
        causal = lax.broadcasted_iota(jnp.int32, (chunk, chunk), 0) >= lax.broadcasted_iota(
            jnp.int32, (chunk, chunk), 1
        )
        scores = jnp.einsum("ktgn,ksgn->kgts", c_part, b_part, preferred_element_type=f32)
        gaps = cum[..., :, None] - cum[..., None, :]
        decays = jnp.exp(jnp.where(causal, gaps, -jnp.inf))
        mixing = decays * jnp.transpose(scores, (1, 0, 2, 3))[:, None] * steps[..., None, :]
        output = jnp.einsum("gjkts,ksgjp->ktgjp", mixing, values32, precision=exact)
        output = output + d_skip.reshape(group_count, per_group)[None, None, :, :, None] * values32

        if nck == 1:
            return output
        later = jnp.stack(local_list[1:], axis=0)
        carried_local = jnp.einsum("ktgn,kgjpn->ktgjp", c_part[1:].astype(f32), later, precision=exact)
        scale = jnp.transpose(jnp.exp(cum[:, :, 1:]), (2, 3, 0, 1))[..., None]
        return jnp.concatenate([output[:1], output[1:] + scale * carried_local], axis=0)

    lo = lax.axis_index("fl")
    hi = lax.axis_index("fh")
    pair_count = seq_count // 2
    half = per_group // 2
    swap = [(0, 1), (1, 0)]
    partner_log = lax.ppermute(dev_log, "fl", swap)
    first_log = jnp.where(lo == 0, dev_log, partner_log)
    second_log = jnp.where(lo == 0, partner_log, dev_log)
    own_half = lax.dynamic_slice_in_dim(dev_state, lo * half, half, axis=1)
    other_half = lax.dynamic_slice_in_dim(dev_state, (1 - lo) * half, half, axis=1)
    recv_a = lax.ppermute(other_half, "fl", swap)
    first_state = jnp.where(lo == 0, own_half, recv_a)
    second_state = jnp.where(lo == 0, recv_a, own_half)
    second_log_half = lax.dynamic_slice_in_dim(second_log, lo * half, half, axis=1)
    first_log_half = lax.dynamic_slice_in_dim(first_log, lo * half, half, axis=1)
    pair_state = jnp.exp(second_log_half)[..., None, None] * first_state + second_state
    pair_log_half = first_log_half + second_log_half
    first_size = half - half // 4
    sizes = (first_size, half - first_size)
    starts = (0, first_size)
    c32 = c_part.astype(f32)
    first_decay = jnp.exp(first_log_half)[..., None, None]
    grow = jnp.exp(cum_dev).reshape(group_count, 2, half, nck, chunk)

    def finish(pair_in, q, intra_out):
        part = slice(starts[q], starts[q] + sizes[q])
        own_in = jnp.where(lo == 0, pair_in, first_decay[:, part] * pair_in + recv_a[:, part])
        sent = jnp.where(lo == 0, first_decay[:, part] * pair_in + own_half[:, part], pair_in)
        recv_c = lax.ppermute(sent, "fl", swap)
        incoming = jnp.where(
            lo == 0, jnp.stack([own_in, recv_c], axis=1), jnp.stack([recv_c, own_in], axis=1)
        )
        carried = jnp.einsum("ktgn,ghrpn->ktghrp", c32, incoming, precision=exact)
        scale = jnp.transpose(grow[:, :, part], (3, 4, 0, 1, 2))[..., None]
        base = intra_out.reshape(nck, chunk, group_count, 2, half, HEAD_DIM)[:, :, :, :, part]
        return (base + scale * carried).reshape(row_count, -1)

    first_in, output = exclusive_scan(
        pair_state[:, :first_size], pair_log_half[:, :first_size], hi, pair_count,
        (values32, b_part, c_part, local_list), intra,
    )

    def first_rows(side):
        first_in, output = side
        return finish(first_in, 0, output)

    second_in, first_piece = exclusive_scan(
        pair_state[:, first_size:], pair_log_half[:, first_size:], hi, pair_count,
        (first_in, output), first_rows,
    )
    sent_first = exchange_rows(first_piece, tp_count)
    sent_second = exchange_rows(finish(second_in, 1, output), tp_count)
    rows = row_count // tp_count
    both = [
        piece.reshape(rows, tp_count, group_count, 2, size, HEAD_DIM)
        for piece, size in zip((sent_first, sent_second), sizes)
    ]
    return jnp.concatenate(both, axis=4).reshape(rows, tp_count * head_count * HEAD_DIM)


def exclusive_scan(state, log_decay, mine, count, side, work):
    shape = state.shape
    width = state.shape[-1]
    heads = log_decay.size
    per_head = state.size // heads // width
    log_rows = -(-heads // width)

    def shifted(value, step):
        return lax.ppermute(value, "fh", [(d, d + step) for d in range(count - step)])

    def combine(got, cur):
        scale = jnp.repeat(jnp.exp(cur[-log_rows:].reshape(-1)[:heads]), per_head)[:, None]
        body = scale * got[:-log_rows] + cur[:-log_rows]
        logs = got[-log_rows:] + cur[-log_rows:]
        return jnp.concatenate([body, logs], axis=0)

    flat_log = jnp.pad(log_decay.reshape(-1), (0, log_rows * width - heads)).reshape(log_rows, width)
    first = jnp.concatenate([state.reshape(-1, width), flat_log], axis=0)
    first, side = lax.optimization_barrier((first, side))
    cur = shifted(first, 1)
    done = work(side)
    cur, done = lax.optimization_barrier((cur, done))
    step = 1
    while step < count:
        got = shifted(cur, step)
        cur = jnp.where(mine >= step, combine(got, cur), cur)
        step *= 2
    return cur[:-log_rows].reshape(shape), done


def exchange_rows(merged, tp_count):
    mine = lax.axis_index("tp")
    rows = merged.shape[0] // tp_count
    blocks = merged.reshape(tp_count, rows, merged.shape[1])
    pieces = [None] * tp_count
    for shift in range(tp_count):
        sent = lax.dynamic_index_in_dim(blocks, (mine + shift) % tp_count, 0, keepdims=False)
        if shift == 0:
            got = sent
        else:
            got = lax.ppermute(sent, "tp", [(d, (d + shift) % tp_count) for d in range(tp_count)])
        pieces[shift] = got
    placed = []
    for column in range(tp_count):
        value = pieces[0]
        for shift in range(1, tp_count):
            value = jnp.where((mine - shift) % tp_count == column, pieces[shift], value)
        placed.append(value)
    return jnp.concatenate(placed, axis=1)


def solution(mesh):
    seq_count = mesh.shape["fsdp"]
    tp_count = mesh.shape["tp"]
    grid = Mesh(mesh.devices.reshape(seq_count // 2, 2, tp_count), ("fh", "fl", "tp"))
    in_specs = (
        P(SEQ, "tp", None),
        P("tp", SEQ),
        P(None, "tp", None),
        P("tp", None),
        P("tp"),
        P("tp"),
        P("tp"),
    )
    out_specs = P(SEQ + ("tp",), None)

    def body(*args):
        return shards(*args, seq_count=seq_count, tp_count=tp_count)

    return jax.shard_map(body, mesh=grid, in_specs=in_specs, out_specs=out_specs, check_vma=False)
```

```python
import jax
import jax.numpy as jnp
from jax import lax
from jax.sharding import Mesh, PartitionSpec as P

HEAD_DIM = 64
STATE = 128
SEQ = ("fh", "fl")


def convolve(xbc, conv_weight, conv_bias, seq_count):
    row_count = xbc.shape[0]
    tap_count = conv_weight.shape[0]
    rim = xbc[row_count - (tap_count - 1) :]
    rim_rows = lax.ppermute(rim, SEQ, [(d, d + 1) for d in range(seq_count - 1)])
    padded = jnp.concatenate([rim_rows, xbc], axis=0)
    summed = conv_bias.astype(jnp.float32)[None]
    for k in range(tap_count):
        summed = summed + conv_weight[k].astype(jnp.float32)[None] * padded[
            k : k + row_count
        ].astype(jnp.float32)
    return jax.nn.silu(summed).astype(jnp.bfloat16)


def shards(xbc, dt_raw, conv_weight, conv_bias, dt_bias, a_log, d_skip, seq_count, tp_count):
    row_count, group_count, _ = xbc.shape
    head_count = dt_raw.shape[0]
    per_group = head_count // group_count
    inner_width = per_group * HEAD_DIM
    exact = lax.Precision.HIGHEST
    f32 = jnp.float32

    activated = convolve(xbc, conv_weight, conv_bias, seq_count)
    chunk = min(128, row_count)
    nck = row_count // chunk
    values = activated[:, :, :inner_width].reshape(nck, chunk, group_count, per_group, HEAD_DIM)
    b_part = activated[:, :, inner_width : inner_width + STATE].reshape(nck, chunk, group_count, STATE)
    c_part = activated[:, :, inner_width + STATE :].reshape(nck, chunk, group_count, STATE)

    step_sizes = jax.nn.softplus(dt_raw.astype(f32) + dt_bias[:, None])
    log_rates = -jnp.exp(a_log)[:, None] * step_sizes
    steps = step_sizes.reshape(group_count, per_group, nck, chunk)
    rates = log_rates.reshape(group_count, per_group, nck, chunk)
    cum = jnp.cumsum(rates, axis=3)
    chunk_log = cum[..., -1]

    values32 = values
    weights = jnp.exp(chunk_log[..., None] - cum) * steps
    weighted = values32 * jnp.transpose(weights, (2, 3, 0, 1))[..., None]
    chunk_states = jnp.einsum("ksgn,ksgjp->kgjpn", b_part.astype(f32), weighted, precision=exact)

    running = jnp.zeros_like(chunk_states[0])
    local_list = []
    for k in range(nck):
        local_list.append(running)
        running = jnp.exp(chunk_log[:, :, k])[..., None, None] * running + chunk_states[k]
    dev_state = running
    cum_dev = cum + jnp.concatenate(
        [jnp.zeros_like(chunk_log[..., :1]), jnp.cumsum(chunk_log, axis=2)[..., :-1]], axis=2
    )[..., None]
    dev_log = jnp.sum(chunk_log, axis=2)

    def intra(side):
        values32, b_part, c_part, local_list = side
        causal = lax.broadcasted_iota(jnp.int32, (chunk, chunk), 0) >= lax.broadcasted_iota(
            jnp.int32, (chunk, chunk), 1
        )
        scores = jnp.einsum("ktgn,ksgn->kgts", c_part, b_part, preferred_element_type=f32)
        gaps = cum[..., :, None] - cum[..., None, :]
        decays = jnp.exp(jnp.where(causal, gaps, -jnp.inf))
        mixing = decays * jnp.transpose(scores, (1, 0, 2, 3))[:, None] * steps[..., None, :]
        output = jnp.einsum("gjkts,ksgjp->ktgjp", mixing, values32, precision=exact)
        output = output + d_skip.reshape(group_count, per_group)[None, None, :, :, None] * values32

        if nck == 1:
            return output
        later = jnp.stack(local_list[1:], axis=0)
        carried_local = jnp.einsum("ktgn,kgjpn->ktgjp", c_part[1:].astype(f32), later, precision=exact)
        scale = jnp.transpose(jnp.exp(cum[:, :, 1:]), (2, 3, 0, 1))[..., None]
        return jnp.concatenate([output[:1], output[1:] + scale * carried_local], axis=0)

    lo = lax.axis_index("fl")
    hi = lax.axis_index("fh")
    pair_count = seq_count // 2
    half = per_group // 2
    swap = [(0, 1), (1, 0)]
    partner_log = lax.ppermute(dev_log, "fl", swap)
    first_log = jnp.where(lo == 0, dev_log, partner_log)
    second_log = jnp.where(lo == 0, partner_log, dev_log)
    own_half = lax.dynamic_slice_in_dim(dev_state, lo * half, half, axis=1)
    other_half = lax.dynamic_slice_in_dim(dev_state, (1 - lo) * half, half, axis=1)
    recv_a = lax.ppermute(other_half, "fl", swap)
    first_state = jnp.where(lo == 0, own_half, recv_a)
    second_state = jnp.where(lo == 0, recv_a, own_half)
    second_log_half = lax.dynamic_slice_in_dim(second_log, lo * half, half, axis=1)
    first_log_half = lax.dynamic_slice_in_dim(first_log, lo * half, half, axis=1)
    pair_state = jnp.exp(second_log_half)[..., None, None] * first_state + second_state
    pair_log_half = first_log_half + second_log_half
    first_size = half - half // 4
    sizes = (first_size, half - first_size)
    starts = (0, first_size)
    c32 = c_part.astype(f32)
    first_decay = jnp.exp(first_log_half)[..., None, None]
    grow = jnp.exp(cum_dev).reshape(group_count, 2, half, nck, chunk)
    by_chunk = nck == tp_count

    def finish(pair_in, q, intra_out):
        part = slice(starts[q], starts[q] + sizes[q])
        own_in = jnp.where(lo == 0, pair_in, first_decay[:, part] * pair_in + recv_a[:, part])
        sent = jnp.where(lo == 0, first_decay[:, part] * pair_in + own_half[:, part], pair_in)
        recv_c = lax.ppermute(sent, "fl", swap)
        incoming = jnp.where(
            lo == 0, jnp.stack([own_in, recv_c], axis=1), jnp.stack([recv_c, own_in], axis=1)
        )
        base = intra_out.reshape(nck, chunk, group_count, 2, half, HEAD_DIM)[:, :, :, :, part]
        if by_chunk:
            carried = jnp.einsum("ktgn,ghrpn->kghrpt", c32, incoming, precision=exact)
            scale = jnp.transpose(grow[:, :, part], (3, 0, 1, 2, 4))[:, :, :, :, None, :]
            return jnp.transpose(base, (0, 2, 3, 4, 5, 1)) + scale * carried
        carried = jnp.einsum("ktgn,ghrpn->ktghrp", c32, incoming, precision=exact)
        scale = jnp.transpose(grow[:, :, part], (3, 4, 0, 1, 2))[..., None]
        return (base + scale * carried).reshape(row_count, -1)

    first_in, output = exclusive_scan(
        pair_state[:, :first_size], pair_log_half[:, :first_size], hi, pair_count,
        (values32, b_part, c_part, local_list), intra,
    )

    def first_rows(side):
        first_in, output = side
        return finish(first_in, 0, output)

    second_in, first_piece = exclusive_scan(
        pair_state[:, first_size:], pair_log_half[:, first_size:], hi, pair_count,
        (first_in, output), first_rows,
    )
    second_piece = finish(second_in, 1, output)
    if by_chunk:
        firsts = exchange_chunks(first_piece, tp_count)
        seconds = exchange_chunks(second_piece, tp_count)
        blocks = jnp.stack(
            [jnp.concatenate([a, b], axis=2) for a, b in zip(firsts, seconds)], axis=0
        )
        return jnp.transpose(blocks, (5, 0, 1, 2, 3, 4)).reshape(chunk, tp_count * head_count * HEAD_DIM)
    sent_first = exchange_rows(first_piece, tp_count)
    sent_second = exchange_rows(second_piece, tp_count)
    rows = row_count // tp_count
    both = [
        piece.reshape(rows, tp_count, group_count, 2, size, HEAD_DIM)
        for piece, size in zip((sent_first, sent_second), sizes)
    ]
    return jnp.concatenate(both, axis=4).reshape(rows, tp_count * head_count * HEAD_DIM)


def exclusive_scan(state, log_decay, mine, count, side, work):
    shape = state.shape
    width = state.shape[-1]
    heads = log_decay.size
    per_head = state.size // heads // width
    log_rows = -(-heads // width)

    def shifted(value, step):
        return lax.ppermute(value, "fh", [(d, d + step) for d in range(count - step)])

    def combine(got, cur):
        scale = jnp.repeat(jnp.exp(cur[-log_rows:].reshape(-1)[:heads]), per_head)[:, None]
        body = scale * got[:-log_rows] + cur[:-log_rows]
        logs = got[-log_rows:] + cur[-log_rows:]
        return jnp.concatenate([body, logs], axis=0)

    flat_log = jnp.pad(log_decay.reshape(-1), (0, log_rows * width - heads)).reshape(log_rows, width)
    first = jnp.concatenate([state.reshape(-1, width), flat_log], axis=0)
    first, side = lax.optimization_barrier((first, side))
    cur = shifted(first, 1)
    done = work(side)
    cur, done = lax.optimization_barrier((cur, done))
    step = 1
    while step < count:
        got = shifted(cur, step)
        cur = jnp.where(mine >= step, combine(got, cur), cur)
        step *= 2
    return cur[:-log_rows].reshape(shape), done


def exchange_chunks(piece, tp_count):
    mine = lax.axis_index("tp")
    pieces = [None] * tp_count
    for shift in range(tp_count):
        sent = lax.dynamic_index_in_dim(piece, (mine + shift) % tp_count, 0, keepdims=False)
        if shift == 0:
            pieces[shift] = sent
        else:
            pieces[shift] = lax.ppermute(
                sent, "tp", [(d, (d + shift) % tp_count) for d in range(tp_count)]
            )
    placed = []
    for column in range(tp_count):
        value = pieces[0]
        for shift in range(1, tp_count):
            value = jnp.where((mine - shift) % tp_count == column, pieces[shift], value)
        placed.append(value)
    return placed


def exchange_rows(merged, tp_count):
    mine = lax.axis_index("tp")
    rows = merged.shape[0] // tp_count
    blocks = merged.reshape(tp_count, rows, merged.shape[1])
    pieces = [None] * tp_count
    for shift in range(tp_count):
        sent = lax.dynamic_index_in_dim(blocks, (mine + shift) % tp_count, 0, keepdims=False)
        if shift == 0:
            got = sent
        else:
            got = lax.ppermute(sent, "tp", [(d, (d + shift) % tp_count) for d in range(tp_count)])
        pieces[shift] = got
    placed = []
    for column in range(tp_count):
        value = pieces[0]
        for shift in range(1, tp_count):
            value = jnp.where((mine - shift) % tp_count == column, pieces[shift], value)
        placed.append(value)
    return jnp.concatenate(placed, axis=1)


def solution(mesh):
    seq_count = mesh.shape["fsdp"]
    tp_count = mesh.shape["tp"]
    grid = Mesh(mesh.devices.reshape(seq_count // 2, 2, tp_count), ("fh", "fl", "tp"))
    in_specs = (
        P(SEQ, "tp", None),
        P("tp", SEQ),
        P(None, "tp", None),
        P("tp", None),
        P("tp"),
        P("tp"),
        P("tp"),
    )
    out_specs = P(SEQ + ("tp",), None)

    def body(*args):
        return shards(*args, seq_count=seq_count, tp_count=tp_count)

    return jax.shard_map(body, mesh=grid, in_specs=in_specs, out_specs=out_specs, check_vma=False)
```

```python
import jax
import jax.numpy as jnp
from jax import lax
from jax.sharding import Mesh, PartitionSpec as P

HEAD_DIM = 64
STATE = 128
SEQ = ("fh", "fl")


def convolve(xbc, conv_weight, conv_bias, seq_count):
    row_count = xbc.shape[0]
    tap_count = conv_weight.shape[0]
    rim = xbc[row_count - (tap_count - 1) :]
    rim_rows = lax.ppermute(rim, SEQ, [(d, d + 1) for d in range(seq_count - 1)])
    padded = jnp.concatenate([rim_rows, xbc], axis=0)
    summed = conv_bias.astype(jnp.float32)[None]
    for k in range(tap_count):
        summed = summed + conv_weight[k].astype(jnp.float32)[None] * padded[
            k : k + row_count
        ].astype(jnp.float32)
    return jax.nn.silu(summed).astype(jnp.bfloat16)


def shards(xbc, dt_raw, conv_weight, conv_bias, dt_bias, a_log, d_skip, seq_count, tp_count):
    row_count, group_count, _ = xbc.shape
    head_count = dt_raw.shape[0]
    per_group = head_count // group_count
    inner_width = per_group * HEAD_DIM
    exact = lax.Precision.HIGHEST
    f32 = jnp.float32

    activated = convolve(xbc, conv_weight, conv_bias, seq_count)
    chunk = min(128, row_count)
    nck = row_count // chunk
    values = activated[:, :, :inner_width].reshape(nck, chunk, group_count, per_group, HEAD_DIM)
    b_part = activated[:, :, inner_width : inner_width + STATE].reshape(nck, chunk, group_count, STATE)
    c_part = activated[:, :, inner_width + STATE :].reshape(nck, chunk, group_count, STATE)

    step_sizes = jax.nn.softplus(dt_raw.astype(f32) + dt_bias[:, None])
    log_rates = -jnp.exp(a_log)[:, None] * step_sizes
    steps = step_sizes.reshape(group_count, per_group, nck, chunk)
    rates = log_rates.reshape(group_count, per_group, nck, chunk)
    cum = jnp.cumsum(rates, axis=3)
    chunk_log = cum[..., -1]

    values32 = values
    weights = jnp.exp(chunk_log[..., None] - cum) * steps
    weighted = values32 * jnp.transpose(weights, (2, 3, 0, 1))[..., None]
    chunk_states = jnp.einsum("ksgn,ksgjp->kgjpn", b_part.astype(f32), weighted, precision=exact)

    running = jnp.zeros_like(chunk_states[0])
    local_list = []
    for k in range(nck):
        local_list.append(running)
        running = jnp.exp(chunk_log[:, :, k])[..., None, None] * running + chunk_states[k]
    dev_state = running
    cum_dev = cum + jnp.concatenate(
        [jnp.zeros_like(chunk_log[..., :1]), jnp.cumsum(chunk_log, axis=2)[..., :-1]], axis=2
    )[..., None]
    dev_log = jnp.sum(chunk_log, axis=2)

    def intra(side):
        values32, b_part, c_part, local_list = side
        causal = lax.broadcasted_iota(jnp.int32, (chunk, chunk), 0) >= lax.broadcasted_iota(
            jnp.int32, (chunk, chunk), 1
        )
        scores = jnp.einsum("ktgn,ksgn->kgts", c_part, b_part, preferred_element_type=f32)
        gaps = cum[..., :, None] - cum[..., None, :]
        decays = jnp.exp(jnp.where(causal, gaps, -jnp.inf))
        mixing = decays * jnp.transpose(scores, (1, 0, 2, 3))[:, None] * steps[..., None, :]
        output = jnp.einsum("gjkts,ksgjp->ktgjp", mixing, values32, precision=exact)
        output = output + d_skip.reshape(group_count, per_group)[None, None, :, :, None] * values32

        if nck == 1:
            return output
        later = jnp.stack(local_list[1:], axis=0)
        carried_local = jnp.einsum("ktgn,kgjpn->ktgjp", c_part[1:].astype(f32), later, precision=exact)
        scale = jnp.transpose(jnp.exp(cum[:, :, 1:]), (2, 3, 0, 1))[..., None]
        return jnp.concatenate([output[:1], output[1:] + scale * carried_local], axis=0)

    lo = lax.axis_index("fl")
    pair_count = seq_count // 2
    half = per_group // 2
    swap = [(0, 1), (1, 0)]
    partner_log = lax.ppermute(dev_log, "fl", swap)
    first_log = jnp.where(lo == 0, dev_log, partner_log)
    second_log = jnp.where(lo == 0, partner_log, dev_log)
    own_half = lax.dynamic_slice_in_dim(dev_state, lo * half, half, axis=1)
    other_half = lax.dynamic_slice_in_dim(dev_state, (1 - lo) * half, half, axis=1)
    recv_a = lax.ppermute(other_half, "fl", swap)
    first_state = jnp.where(lo == 0, own_half, recv_a)
    second_state = jnp.where(lo == 0, recv_a, own_half)
    second_log_half = lax.dynamic_slice_in_dim(second_log, lo * half, half, axis=1)
    first_log_half = lax.dynamic_slice_in_dim(first_log, lo * half, half, axis=1)
    pair_state = jnp.exp(second_log_half)[..., None, None] * first_state + second_state
    pair_log_half = first_log_half + second_log_half
    first_size = half - half // 4
    sizes = (first_size, half - first_size)
    starts = (0, first_size)
    c32 = c_part.astype(f32)
    first_decay = jnp.exp(first_log_half)[..., None, None]
    grow = jnp.exp(cum_dev).reshape(group_count, 2, half, nck, chunk)
    by_chunk = nck == tp_count

    def finish(pair_in, q, intra_out):
        part = slice(starts[q], starts[q] + sizes[q])
        own_in = jnp.where(lo == 0, pair_in, first_decay[:, part] * pair_in + recv_a[:, part])
        sent = jnp.where(lo == 0, first_decay[:, part] * pair_in + own_half[:, part], pair_in)
        recv_c = lax.ppermute(sent, "fl", swap)
        incoming = jnp.where(
            lo == 0, jnp.stack([own_in, recv_c], axis=1), jnp.stack([recv_c, own_in], axis=1)
        )
        base = intra_out.reshape(nck, chunk, group_count, 2, half, HEAD_DIM)[:, :, :, :, part]
        if by_chunk:
            carried = jnp.einsum("ktgn,ghrpn->kghrpt", c32, incoming, precision=exact)
            scale = jnp.transpose(grow[:, :, part], (3, 0, 1, 2, 4))[:, :, :, :, None, :]
            return jnp.transpose(base, (0, 2, 3, 4, 5, 1)) + scale * carried
        carried = jnp.einsum("ktgn,ghrpn->ktghrp", c32, incoming, precision=exact)
        scale = jnp.transpose(grow[:, :, part], (3, 4, 0, 1, 2))[..., None]
        return (base + scale * carried).reshape(row_count, -1)

    first_in, output = exclusive_scan(
        pair_state[:, :first_size], pair_log_half[:, :first_size], pair_count,
        (values32, b_part, c_part, local_list), intra,
    )

    def first_rows(side):
        first_in, output = side
        return finish(first_in, 0, output)

    second_in, first_piece = exclusive_scan(
        pair_state[:, first_size:], pair_log_half[:, first_size:], pair_count,
        (first_in, output), first_rows,
    )
    second_piece = finish(second_in, 1, output)
    if by_chunk:
        firsts = exchange_chunks(first_piece, tp_count)
        seconds = exchange_chunks(second_piece, tp_count)
        blocks = jnp.stack(
            [jnp.concatenate([a, b], axis=2) for a, b in zip(firsts, seconds)], axis=0
        )
        return jnp.transpose(blocks, (5, 0, 1, 2, 3, 4)).reshape(chunk, tp_count * head_count * HEAD_DIM)
    sent_first = exchange_rows(first_piece, tp_count)
    sent_second = exchange_rows(second_piece, tp_count)
    rows = row_count // tp_count
    both = [
        piece.reshape(rows, tp_count, group_count, 2, size, HEAD_DIM)
        for piece, size in zip((sent_first, sent_second), sizes)
    ]
    return jnp.concatenate(both, axis=4).reshape(rows, tp_count * head_count * HEAD_DIM)


def exclusive_scan(state, log_decay, count, side, work):
    shape = state.shape
    width = state.shape[-1]
    heads = log_decay.size
    per_head = state.size // heads // width
    log_rows = -(-heads // width)

    def shifted(value, step):
        return lax.ppermute(value, "fh", [(d, d + step) for d in range(count - step)])

    def combine(got, cur):
        scale = jnp.repeat(jnp.exp(cur[-log_rows:].reshape(-1)[:heads]), per_head)[:, None]
        body = scale * got[:-log_rows] + cur[:-log_rows]
        logs = got[-log_rows:] + cur[-log_rows:]
        return jnp.concatenate([body, logs], axis=0)

    flat_log = jnp.pad(log_decay.reshape(-1), (0, log_rows * width - heads)).reshape(log_rows, width)
    first = jnp.concatenate([state.reshape(-1, width), flat_log], axis=0)
    first, side = lax.optimization_barrier((first, side))
    cur = shifted(first, 1)
    done = work(side)
    cur, done = lax.optimization_barrier((cur, done))
    window = combine(cur, first)
    step = 2
    while step < count:
        got = shifted(window, step)
        cur = combine(got, cur)
        if 2 * step < count:
            window = combine(got, window)
        step *= 2
    return cur[:-log_rows].reshape(shape), done


def exchange_chunks(piece, tp_count):
    mine = lax.axis_index("tp")
    pieces = [None] * tp_count
    for shift in range(tp_count):
        sent = lax.dynamic_index_in_dim(piece, (mine + shift) % tp_count, 0, keepdims=False)
        if shift == 0:
            pieces[shift] = sent
        else:
            pieces[shift] = lax.ppermute(
                sent, "tp", [(d, (d + shift) % tp_count) for d in range(tp_count)]
            )
    placed = []
    for column in range(tp_count):
        value = pieces[0]
        for shift in range(1, tp_count):
            value = jnp.where((mine - shift) % tp_count == column, pieces[shift], value)
        placed.append(value)
    return placed


def exchange_rows(merged, tp_count):
    mine = lax.axis_index("tp")
    rows = merged.shape[0] // tp_count
    blocks = merged.reshape(tp_count, rows, merged.shape[1])
    pieces = [None] * tp_count
    for shift in range(tp_count):
        sent = lax.dynamic_index_in_dim(blocks, (mine + shift) % tp_count, 0, keepdims=False)
        if shift == 0:
            got = sent
        else:
            got = lax.ppermute(sent, "tp", [(d, (d + shift) % tp_count) for d in range(tp_count)])
        pieces[shift] = got
    placed = []
    for column in range(tp_count):
        value = pieces[0]
        for shift in range(1, tp_count):
            value = jnp.where((mine - shift) % tp_count == column, pieces[shift], value)
        placed.append(value)
    return jnp.concatenate(placed, axis=1)


def solution(mesh):
    seq_count = mesh.shape["fsdp"]
    tp_count = mesh.shape["tp"]
    grid = Mesh(mesh.devices.reshape(seq_count // 2, 2, tp_count), ("fh", "fl", "tp"))
    in_specs = (
        P(SEQ, "tp", None),
        P("tp", SEQ),
        P(None, "tp", None),
        P("tp", None),
        P("tp"),
        P("tp"),
        P("tp"),
    )
    out_specs = P(SEQ + ("tp",), None)

    def body(*args):
        return shards(*args, seq_count=seq_count, tp_count=tp_count)

    return jax.shard_map(body, mesh=grid, in_specs=in_specs, out_specs=out_specs, check_vma=False)
```

```python
import jax
import jax.numpy as jnp
from jax import lax
from jax.sharding import Mesh, PartitionSpec as P

HEAD_DIM = 64
STATE = 128
SEQ = ("fh", "fl")


def convolve(xbc, conv_weight, conv_bias, seq_count):
    row_count = xbc.shape[0]
    tap_count = conv_weight.shape[0]
    rim = xbc[row_count - (tap_count - 1) :]
    rim_rows = lax.ppermute(rim, SEQ, [(d, d + 1) for d in range(seq_count - 1)])
    padded = jnp.concatenate([rim_rows, xbc], axis=0)
    summed = conv_bias.astype(jnp.float32)[None]
    for k in range(tap_count):
        summed = summed + conv_weight[k].astype(jnp.float32)[None] * padded[
            k : k + row_count
        ].astype(jnp.float32)
    return jax.nn.silu(summed).astype(jnp.bfloat16)


def shards(xbc, dt_raw, conv_weight, conv_bias, dt_bias, a_log, d_skip, seq_count, tp_count):
    row_count, group_count, _ = xbc.shape
    head_count = dt_raw.shape[0]
    per_group = head_count // group_count
    inner_width = per_group * HEAD_DIM
    exact = lax.Precision.HIGHEST
    f32 = jnp.float32

    activated = convolve(xbc, conv_weight, conv_bias, seq_count)
    chunk = min(128, row_count)
    nck = row_count // chunk
    values = activated[:, :, :inner_width].reshape(nck, chunk, group_count, per_group, HEAD_DIM)
    b_part = activated[:, :, inner_width : inner_width + STATE].reshape(nck, chunk, group_count, STATE)
    c_part = activated[:, :, inner_width + STATE :].reshape(nck, chunk, group_count, STATE)

    step_sizes = jax.nn.softplus(dt_raw.astype(f32) + dt_bias[:, None])
    log_rates = -jnp.exp(a_log)[:, None] * step_sizes
    steps = step_sizes.reshape(group_count, per_group, nck, chunk)
    rates = log_rates.reshape(group_count, per_group, nck, chunk)
    cum = jnp.cumsum(rates, axis=3)
    chunk_log = cum[..., -1]

    values32 = values
    weights = jnp.exp(chunk_log[..., None] - cum) * steps
    weighted = values32 * jnp.transpose(weights, (2, 3, 0, 1))[..., None]
    chunk_states = jnp.einsum("ksgn,ksgjp->kgjpn", b_part.astype(f32), weighted, precision=exact)

    running = jnp.zeros_like(chunk_states[0])
    local_list = []
    for k in range(nck):
        local_list.append(running)
        running = jnp.exp(chunk_log[:, :, k])[..., None, None] * running + chunk_states[k]
    dev_state = running
    cum_dev = cum + jnp.concatenate(
        [jnp.zeros_like(chunk_log[..., :1]), jnp.cumsum(chunk_log, axis=2)[..., :-1]], axis=2
    )[..., None]
    dev_log = jnp.sum(chunk_log, axis=2)

    def intra(side):
        values32, b_part, c_part, local_list = side
        causal = lax.broadcasted_iota(jnp.int32, (chunk, chunk), 0) >= lax.broadcasted_iota(
            jnp.int32, (chunk, chunk), 1
        )
        scores = jnp.einsum("ktgn,ksgn->kgts", c_part, b_part, preferred_element_type=f32)
        gaps = cum[..., :, None] - cum[..., None, :]
        decays = jnp.exp(jnp.where(causal, gaps, -jnp.inf))
        mixing = decays * jnp.transpose(scores, (1, 0, 2, 3))[:, None] * steps[..., None, :]
        output = jnp.einsum("gjkts,ksgjp->ktgjp", mixing, values32, precision=exact)
        output = output + d_skip.reshape(group_count, per_group)[None, None, :, :, None] * values32

        if nck == 1:
            return output
        later = jnp.stack(local_list[1:], axis=0)
        carried_local = jnp.einsum("ktgn,kgjpn->ktgjp", c_part[1:].astype(f32), later, precision=exact)
        scale = jnp.transpose(jnp.exp(cum[:, :, 1:]), (2, 3, 0, 1))[..., None]
        return jnp.concatenate([output[:1], output[1:] + scale * carried_local], axis=0)

    lo = lax.axis_index("fl")
    pair_count = seq_count // 2
    half = per_group // 2
    swap = [(0, 1), (1, 0)]
    partner_log = lax.ppermute(dev_log, "fl", swap)
    first_log = jnp.where(lo == 0, dev_log, partner_log)
    second_log = jnp.where(lo == 0, partner_log, dev_log)
    own_half = lax.dynamic_slice_in_dim(dev_state, lo * half, half, axis=1)
    other_half = lax.dynamic_slice_in_dim(dev_state, (1 - lo) * half, half, axis=1)
    recv_a = lax.ppermute(other_half, "fl", swap)
    first_state = jnp.where(lo == 0, own_half, recv_a)
    second_state = jnp.where(lo == 0, recv_a, own_half)
    second_log_half = lax.dynamic_slice_in_dim(second_log, lo * half, half, axis=1)
    first_log_half = lax.dynamic_slice_in_dim(first_log, lo * half, half, axis=1)
    pair_state = jnp.exp(second_log_half)[..., None, None] * first_state + second_state
    pair_log_half = first_log_half + second_log_half
    first_size = half - half // 4
    sizes = (first_size, half - first_size)
    starts = (0, first_size)
    c32 = c_part.astype(f32)
    first_decay = jnp.exp(first_log_half)[..., None, None]
    grow = jnp.exp(cum_dev).reshape(group_count, 2, half, nck, chunk)
    by_chunk = nck == tp_count

    def finish(pair_in, q, intra_out):
        part = slice(starts[q], starts[q] + sizes[q])
        own_in = jnp.where(lo == 0, pair_in, first_decay[:, part] * pair_in + recv_a[:, part])
        sent = jnp.where(lo == 0, first_decay[:, part] * pair_in + own_half[:, part], pair_in)
        recv_c = lax.ppermute(sent, "fl", swap)
        incoming = jnp.where(
            lo == 0, jnp.stack([own_in, recv_c], axis=1), jnp.stack([recv_c, own_in], axis=1)
        )
        base = intra_out.reshape(nck, chunk, group_count, 2, half, HEAD_DIM)[:, :, :, :, part]
        if by_chunk:
            carried = jnp.einsum("ktgn,ghrpn->kghrpt", c32, incoming, precision=lax.Precision.HIGH)
            scale = jnp.transpose(grow[:, :, part], (3, 0, 1, 2, 4))[:, :, :, :, None, :]
            return jnp.transpose(base, (0, 2, 3, 4, 5, 1)) + scale * carried
        carried = jnp.einsum("ktgn,ghrpn->ktghrp", c32, incoming, precision=lax.Precision.HIGH)
        scale = jnp.transpose(grow[:, :, part], (3, 4, 0, 1, 2))[..., None]
        return (base + scale * carried).reshape(row_count, -1)

    first_in, output = exclusive_scan(
        pair_state[:, :first_size], pair_log_half[:, :first_size], pair_count,
        (values32, b_part, c_part, local_list), intra,
    )

    def first_rows(side):
        first_in, output = side
        return finish(first_in, 0, output)

    second_in, first_piece = exclusive_scan(
        pair_state[:, first_size:], pair_log_half[:, first_size:], pair_count,
        (first_in, output), first_rows,
    )
    second_piece = finish(second_in, 1, output)
    if by_chunk:
        firsts = exchange_chunks(first_piece, tp_count)
        seconds = exchange_chunks(second_piece, tp_count)
        mine = lax.axis_index("tp")
        by_shift = [jnp.concatenate([a, b], axis=2)[None] for a, b in zip(firsts, seconds)]
        column = lax.broadcasted_iota(jnp.int32, (tp_count,) + (1,) * (by_shift[0].ndim - 1), 0)
        blocks = by_shift[0]
        for shift in range(1, tp_count):
            blocks = jnp.where((mine - shift) % tp_count == column, by_shift[shift], blocks)
        return jnp.transpose(blocks, (5, 0, 1, 2, 3, 4)).reshape(chunk, tp_count * head_count * HEAD_DIM)
    sent_first = exchange_rows(first_piece, tp_count)
    sent_second = exchange_rows(second_piece, tp_count)
    rows = row_count // tp_count
    both = [
        piece.reshape(rows, tp_count, group_count, 2, size, HEAD_DIM)
        for piece, size in zip((sent_first, sent_second), sizes)
    ]
    return jnp.concatenate(both, axis=4).reshape(rows, tp_count * head_count * HEAD_DIM)


def exclusive_scan(state, log_decay, count, side, work):
    shape = state.shape
    width = state.shape[-1]
    heads = log_decay.size
    per_head = state.size // heads // width
    log_rows = -(-heads // width)

    def shifted(value, step):
        return lax.ppermute(value, "fh", [(d, d + step) for d in range(count - step)])

    def combine(got, cur):
        scale = jnp.repeat(jnp.exp(cur[-log_rows:].reshape(-1)[:heads]), per_head)[:, None]
        body = scale * got[:-log_rows] + cur[:-log_rows]
        logs = got[-log_rows:] + cur[-log_rows:]
        return jnp.concatenate([body, logs], axis=0)

    flat_log = jnp.pad(log_decay.reshape(-1), (0, log_rows * width - heads)).reshape(log_rows, width)
    first = jnp.concatenate([state.reshape(-1, width), flat_log], axis=0)
    first, side = lax.optimization_barrier((first, side))
    cur = shifted(first, 1)
    done = work(side)
    cur, done = lax.optimization_barrier((cur, done))
    window = combine(cur, first)
    step = 2
    while step < count:
        got = shifted(window, step)
        cur = combine(got, cur)
        if 2 * step < count:
            window = combine(got, window)
        step *= 2
    return cur[:-log_rows].reshape(shape), done


def exchange_chunks(piece, tp_count):
    mine = lax.axis_index("tp")
    pieces = [None] * tp_count
    for shift in range(tp_count):
        sent = lax.dynamic_index_in_dim(piece, (mine + shift) % tp_count, 0, keepdims=False)
        if shift == 0:
            pieces[shift] = sent
        else:
            pieces[shift] = lax.ppermute(
                sent, "tp", [(d, (d + shift) % tp_count) for d in range(tp_count)]
            )
    return pieces


def exchange_rows(merged, tp_count):
    mine = lax.axis_index("tp")
    rows = merged.shape[0] // tp_count
    blocks = merged.reshape(tp_count, rows, merged.shape[1])
    pieces = [None] * tp_count
    for shift in range(tp_count):
        sent = lax.dynamic_index_in_dim(blocks, (mine + shift) % tp_count, 0, keepdims=False)
        if shift == 0:
            got = sent
        else:
            got = lax.ppermute(sent, "tp", [(d, (d + shift) % tp_count) for d in range(tp_count)])
        pieces[shift] = got
    placed = []
    for column in range(tp_count):
        value = pieces[0]
        for shift in range(1, tp_count):
            value = jnp.where((mine - shift) % tp_count == column, pieces[shift], value)
        placed.append(value)
    return jnp.concatenate(placed, axis=1)


def solution(mesh):
    seq_count = mesh.shape["fsdp"]
    tp_count = mesh.shape["tp"]
    grid = Mesh(mesh.devices.reshape(seq_count // 2, 2, tp_count), ("fh", "fl", "tp"))
    in_specs = (
        P(SEQ, "tp", None),
        P("tp", SEQ),
        P(None, "tp", None),
        P("tp", None),
        P("tp"),
        P("tp"),
        P("tp"),
    )
    out_specs = P(SEQ + ("tp",), None)

    def body(*args):
        return shards(*args, seq_count=seq_count, tp_count=tp_count)

    return jax.shard_map(body, mesh=grid, in_specs=in_specs, out_specs=out_specs, check_vma=False)
```

```python
import jax
import jax.numpy as jnp
from jax import lax
from jax.sharding import Mesh, PartitionSpec as P

HEAD_DIM = 64
STATE = 128
SEQ = ("fh", "fl")


def convolve(xbc, conv_weight, conv_bias, seq_count):
    row_count = xbc.shape[0]
    tap_count = conv_weight.shape[0]
    rim = xbc[row_count - (tap_count - 1) :]
    rim_rows = lax.ppermute(rim, SEQ, [(d, d + 1) for d in range(seq_count - 1)])
    padded = jnp.concatenate([rim_rows, xbc], axis=0)
    summed = conv_bias.astype(jnp.float32)[None]
    for k in range(tap_count):
        summed = summed + conv_weight[k].astype(jnp.float32)[None] * padded[
            k : k + row_count
        ].astype(jnp.float32)
    return jax.nn.silu(summed).astype(jnp.bfloat16)


def shards(xbc, dt_raw, conv_weight, conv_bias, dt_bias, a_log, d_skip, seq_count, tp_count):
    row_count, group_count, _ = xbc.shape
    head_count = dt_raw.shape[0]
    per_group = head_count // group_count
    inner_width = per_group * HEAD_DIM
    exact = lax.Precision.HIGHEST
    f32 = jnp.float32

    activated = convolve(xbc, conv_weight, conv_bias, seq_count)
    chunk = min(128, row_count)
    nck = row_count // chunk
    values = activated[:, :, :inner_width].reshape(nck, chunk, group_count, per_group, HEAD_DIM)
    b_part = activated[:, :, inner_width : inner_width + STATE].reshape(nck, chunk, group_count, STATE)
    c_part = activated[:, :, inner_width + STATE :].reshape(nck, chunk, group_count, STATE)

    step_sizes = jax.nn.softplus(dt_raw.astype(f32) + dt_bias[:, None])
    log_rates = -jnp.exp(a_log)[:, None] * step_sizes
    steps = step_sizes.reshape(group_count, per_group, nck, chunk)
    rates = log_rates.reshape(group_count, per_group, nck, chunk)
    cum = jnp.cumsum(rates, axis=3)
    chunk_log = cum[..., -1]

    values32 = values
    weights = jnp.exp(chunk_log[..., None] - cum) * steps
    weighted = values32 * jnp.transpose(weights, (2, 3, 0, 1))[..., None]
    chunk_states = jnp.einsum("ksgn,ksgjp->kgjpn", b_part.astype(f32), weighted, precision=lax.Precision.HIGH)

    running = jnp.zeros_like(chunk_states[0])
    local_list = []
    for k in range(nck):
        local_list.append(running)
        running = jnp.exp(chunk_log[:, :, k])[..., None, None] * running + chunk_states[k]
    dev_state = running
    cum_dev = cum + jnp.concatenate(
        [jnp.zeros_like(chunk_log[..., :1]), jnp.cumsum(chunk_log, axis=2)[..., :-1]], axis=2
    )[..., None]
    dev_log = jnp.sum(chunk_log, axis=2)

    def intra(side):
        values32, b_part, c_part, local_list = side
        causal = lax.broadcasted_iota(jnp.int32, (chunk, chunk), 0) >= lax.broadcasted_iota(
            jnp.int32, (chunk, chunk), 1
        )
        scores = jnp.einsum("ktgn,ksgn->kgts", c_part, b_part, preferred_element_type=f32)
        gaps = cum[..., :, None] - cum[..., None, :]
        decays = jnp.exp(jnp.where(causal, gaps, -jnp.inf))
        mixing = decays * jnp.transpose(scores, (1, 0, 2, 3))[:, None] * steps[..., None, :]
        output = jnp.einsum("gjkts,ksgjp->ktgjp", mixing, values32, precision=exact)
        output = output + d_skip.reshape(group_count, per_group)[None, None, :, :, None] * values32

        if nck == 1:
            return output
        later = jnp.stack(local_list[1:], axis=0)
        carried_local = jnp.einsum("ktgn,kgjpn->ktgjp", c_part[1:].astype(f32), later, precision=exact)
        scale = jnp.transpose(jnp.exp(cum[:, :, 1:]), (2, 3, 0, 1))[..., None]
        return jnp.concatenate([output[:1], output[1:] + scale * carried_local], axis=0)

    lo = lax.axis_index("fl")
    pair_count = seq_count // 2
    half = per_group // 2
    swap = [(0, 1), (1, 0)]
    partner_log = lax.ppermute(dev_log, "fl", swap)
    first_log = jnp.where(lo == 0, dev_log, partner_log)
    second_log = jnp.where(lo == 0, partner_log, dev_log)
    own_half = lax.dynamic_slice_in_dim(dev_state, lo * half, half, axis=1)
    other_half = lax.dynamic_slice_in_dim(dev_state, (1 - lo) * half, half, axis=1)
    recv_a = lax.ppermute(other_half, "fl", swap)
    first_state = jnp.where(lo == 0, own_half, recv_a)
    second_state = jnp.where(lo == 0, recv_a, own_half)
    second_log_half = lax.dynamic_slice_in_dim(second_log, lo * half, half, axis=1)
    first_log_half = lax.dynamic_slice_in_dim(first_log, lo * half, half, axis=1)
    pair_state = jnp.exp(second_log_half)[..., None, None] * first_state + second_state
    pair_log_half = first_log_half + second_log_half
    first_size = half - half // 4
    sizes = (first_size, half - first_size)
    starts = (0, first_size)
    c32 = c_part.astype(f32)
    first_decay = jnp.exp(first_log_half)[..., None, None]
    grow = jnp.exp(cum_dev).reshape(group_count, 2, half, nck, chunk)
    by_chunk = nck == tp_count

    def finish(pair_in, q, intra_out):
        part = slice(starts[q], starts[q] + sizes[q])
        own_in = jnp.where(lo == 0, pair_in, first_decay[:, part] * pair_in + recv_a[:, part])
        sent = jnp.where(lo == 0, first_decay[:, part] * pair_in + own_half[:, part], pair_in)
        recv_c = lax.ppermute(sent, "fl", swap)
        incoming = jnp.where(
            lo == 0, jnp.stack([own_in, recv_c], axis=1), jnp.stack([recv_c, own_in], axis=1)
        )
        base = intra_out.reshape(nck, chunk, group_count, 2, half, HEAD_DIM)[:, :, :, :, part]
        if by_chunk:
            carried = jnp.einsum("ktgn,ghrpn->kghrpt", c32, incoming, precision=exact)
            scale = jnp.transpose(grow[:, :, part], (3, 0, 1, 2, 4))[:, :, :, :, None, :]
            return jnp.transpose(base, (0, 2, 3, 4, 5, 1)) + scale * carried
        carried = jnp.einsum("ktgn,ghrpn->ktghrp", c32, incoming, precision=exact)
        scale = jnp.transpose(grow[:, :, part], (3, 4, 0, 1, 2))[..., None]
        return (base + scale * carried).reshape(row_count, -1)

    first_in, output = exclusive_scan(
        pair_state[:, :first_size], pair_log_half[:, :first_size], pair_count,
        (values32, b_part, c_part, local_list), intra,
    )

    def first_rows(side):
        first_in, output = side
        return finish(first_in, 0, output)

    second_in, first_piece = exclusive_scan(
        pair_state[:, first_size:], pair_log_half[:, first_size:], pair_count,
        (first_in, output), first_rows,
    )
    second_piece = finish(second_in, 1, output)
    if by_chunk:
        firsts = exchange_chunks(first_piece, tp_count)
        seconds = exchange_chunks(second_piece, tp_count)
        mine = lax.axis_index("tp")
        by_shift = [jnp.concatenate([a, b], axis=2)[None] for a, b in zip(firsts, seconds)]
        column = lax.broadcasted_iota(jnp.int32, (tp_count,) + (1,) * (by_shift[0].ndim - 1), 0)
        blocks = by_shift[0]
        for shift in range(1, tp_count):
            blocks = jnp.where((mine - shift) % tp_count == column, by_shift[shift], blocks)
        return jnp.transpose(blocks, (5, 0, 1, 2, 3, 4)).reshape(chunk, tp_count * head_count * HEAD_DIM)
    sent_first = exchange_rows(first_piece, tp_count)
    sent_second = exchange_rows(second_piece, tp_count)
    rows = row_count // tp_count
    both = [
        piece.reshape(rows, tp_count, group_count, 2, size, HEAD_DIM)
        for piece, size in zip((sent_first, sent_second), sizes)
    ]
    return jnp.concatenate(both, axis=4).reshape(rows, tp_count * head_count * HEAD_DIM)


def exclusive_scan(state, log_decay, count, side, work):
    shape = state.shape
    width = state.shape[-1]
    heads = log_decay.size
    per_head = state.size // heads // width
    log_rows = -(-heads // width)

    def shifted(value, step):
        return lax.ppermute(value, "fh", [(d, d + step) for d in range(count - step)])

    def combine(got, cur):
        scale = jnp.repeat(jnp.exp(cur[-log_rows:].reshape(-1)[:heads]), per_head)[:, None]
        body = scale * got[:-log_rows] + cur[:-log_rows]
        logs = got[-log_rows:] + cur[-log_rows:]
        return jnp.concatenate([body, logs], axis=0)

    flat_log = jnp.pad(log_decay.reshape(-1), (0, log_rows * width - heads)).reshape(log_rows, width)
    first = jnp.concatenate([state.reshape(-1, width), flat_log], axis=0)
    first, side = lax.optimization_barrier((first, side))
    cur = shifted(first, 1)
    done = work(side)
    cur, done = lax.optimization_barrier((cur, done))
    window = combine(cur, first)
    step = 2
    while step < count:
        got = shifted(window, step)
        cur = combine(got, cur)
        if 2 * step < count:
            window = combine(got, window)
        step *= 2
    return cur[:-log_rows].reshape(shape), done


def exchange_chunks(piece, tp_count):
    mine = lax.axis_index("tp")
    pieces = [None] * tp_count
    for shift in range(tp_count):
        sent = lax.dynamic_index_in_dim(piece, (mine + shift) % tp_count, 0, keepdims=False)
        if shift == 0:
            pieces[shift] = sent
        else:
            pieces[shift] = lax.ppermute(
                sent, "tp", [(d, (d + shift) % tp_count) for d in range(tp_count)]
            )
    return pieces


def exchange_rows(merged, tp_count):
    mine = lax.axis_index("tp")
    rows = merged.shape[0] // tp_count
    blocks = merged.reshape(tp_count, rows, merged.shape[1])
    pieces = [None] * tp_count
    for shift in range(tp_count):
        sent = lax.dynamic_index_in_dim(blocks, (mine + shift) % tp_count, 0, keepdims=False)
        if shift == 0:
            got = sent
        else:
            got = lax.ppermute(sent, "tp", [(d, (d + shift) % tp_count) for d in range(tp_count)])
        pieces[shift] = got
    placed = []
    for column in range(tp_count):
        value = pieces[0]
        for shift in range(1, tp_count):
            value = jnp.where((mine - shift) % tp_count == column, pieces[shift], value)
        placed.append(value)
    return jnp.concatenate(placed, axis=1)


def solution(mesh):
    seq_count = mesh.shape["fsdp"]
    tp_count = mesh.shape["tp"]
    grid = Mesh(mesh.devices.reshape(seq_count // 2, 2, tp_count), ("fh", "fl", "tp"))
    in_specs = (
        P(SEQ, "tp", None),
        P("tp", SEQ),
        P(None, "tp", None),
        P("tp", None),
        P("tp"),
        P("tp"),
        P("tp"),
    )
    out_specs = P(SEQ + ("tp",), None)

    def body(*args):
        return shards(*args, seq_count=seq_count, tp_count=tp_count)

    return jax.shard_map(body, mesh=grid, in_specs=in_specs, out_specs=out_specs, check_vma=False)
```
